128 devices in a mesh: rad: 8 (over x, z_lo), azi: 16 (over z_hi, y, core).
Axes of the slice: x: 4, y: 4, z: 4 (z_hi: 2, z_lo: 2; z = z_hi * 2 + z_lo), core: 2. Of those that a mesh axis runs over, the one named last changes fastest.
Arguments:
- fluid_state: float32 [64, 8, 16, 16384], P('rad', None, None, 'azi'), may hold values from -6 to 6
- orbit_shift: int32 [64], P('rad'), may hold values from 0 to 16383
- residual_speed: float32 [64], P('rad'), may hold values from -0.5 to 0.5
- coupling: float32 [8, 8], replicated, may hold values from -1.2 to 1.2
- radial_solve: float32 [8, 64, 64], replicated, as said below
Outputs:
- advanced: float32 [64, 8, 16, 16384], P('rad', None, None, 'azi')
The draws below stay inside these ranges and needn't reach their ends.
Inputs may be any that keep to these rules, and one draw needn't show every extreme that they name: radial_solve is, for each field, a dense block of the inverse of the radial operator over the window's radii, whose entries fall off with the distance of the two radii.
All inputs are finite; a program needn't handle non-finite values.
Results may differ from the reference program's by a relative error of at most 0.0003.
Values sent between devices are 32-bit elements; how exact they have to be, the bound alone decides.
No kernel may reach another device: no remote copies, remote signals or barrier semaphores. Data moves between devices by JAX's collectives and lax.ppermute only.
A program may use at most 128 MiB of HBM per device.

```python
import jax
import jax.numpy as jnp
from jax import lax

FIELDS = 8
PLANES = 16
R_DEV = 8
NR = 64
NPHI = 16384


def draw_radial_solve(key, part):
    length = 2.0 * R_DEV
    first = jnp.arange(NR)[:, None]
    second = jnp.arange(NR)[None, :]
    distance = jnp.abs(first - second).astype(jnp.float32)
    identity = (first == second).astype(jnp.float32)
    noise = jax.random.normal(key, (FIELDS, NR, NR), jnp.float32)
    return (identity + noise / jnp.sqrt(length)) * jnp.exp(-distance / length)


def with_ends(result, rng, low, high):
    spot = [jax.random.randint(jax.random.fold_in(rng, axis), (), 0, length) for axis, length in enumerate(result.shape)]
    main_axis = result.shape.index(max(result.shape))
    neighbour = spot[:main_axis] + [(spot[main_axis] + 1) % result.shape[main_axis]] + spot[main_axis + 1:]
    return result.at[tuple(spot)].set(low).at[tuple(neighbour)].set(high)


def block_scale(rng, extent, pieces, least, high):
    def one(dim, parts):
        steps = jax.random.uniform(jax.random.fold_in(jax.random.fold_in(rng, 6), dim), (parts,), jnp.float32, least / len(pieces), high / len(pieces))
        return jnp.repeat(jnp.exp(steps), extent[dim] // parts).reshape((-1,) + (1,) * (len(extent) - dim - 1))

    factor_of = one(*pieces[0])
    for cut in pieces[1:]:
        factor_of = factor_of * one(*cut)
    return factor_of


def bell_draw(key, dims, width, limit, split=(), held_as=jnp.bfloat16):
    entries = width * jax.random.normal(key, dims, jnp.float32)
    if split:
        entries = entries * block_scale(key, dims, split, -0.22, 0.18)
    return jnp.clip(entries, -limit, limit).astype(held_as)


def setup_inputs(seed: int = 0) -> dict:
    keys = jax.random.split(jax.random.key(seed), 6)
    return {
        "fluid_state": bell_draw(keys[0], (NR, FIELDS, PLANES, NPHI), 1.0, 6.0, ((0, 8), (3, 16)), jnp.float32),
        "orbit_shift": with_ends(jax.random.randint(keys[1], (NR,), 0, NPHI), jax.random.fold_in(keys[1], 1), 0, NPHI - 1).astype(jnp.int32),
        "residual_speed": jnp.clip(jax.random.uniform(keys[2], (NR,), jnp.float32, -0.5, 0.5) * block_scale(keys[2], (NR,), ((0, 8),), -0.4, 0.0), -0.5, 0.5),
        "coupling": bell_draw(keys[3], (FIELDS, FIELDS), 0.2, 1.2, (), jnp.float32),
        "radial_solve": draw_radial_solve(jax.random.fold_in(keys[5], 71), 0),
    }


def face_flux(left, right, speed):
    return 0.5 * speed * (left + right) - 0.5 * jnp.abs(speed) * (right - left)


def reference(fluid_state, orbit_shift, residual_speed, coupling, radial_solve):
    columns = jnp.arange(NPHI, dtype=jnp.int32)

    def remap_row(items):
        row, amount = items
        where = jnp.mod(columns - amount, NPHI).astype(jnp.int32)
        return jnp.take(row, where, axis=2)

    remapped = lax.map(remap_row, (fluid_state, orbit_shift))
    speed = residual_speed[:, None, None, None]
    upper = jnp.roll(remapped, -1, axis=3)
    lower = jnp.roll(remapped, 1, axis=3)
    advected = remapped - (face_flux(remapped, upper, speed) - face_flux(lower, remapped, speed))
    padded = jnp.pad(advected, ((1, 1), (0, 0), (0, 0), (0, 0)))
    explicit = advected + jnp.einsum("fg,rgzj->rfzj", coupling, padded[2:] - padded[:-2], precision=lax.Precision.HIGHEST)
    return jnp.einsum("frk,kfzj->rfzj", radial_solve, explicit, precision=lax.Precision.HIGHEST)
```

```python
import jax
import jax.numpy as jnp
from jax import lax
from jax.experimental import pallas as pl
from jax.experimental.pallas import tpu as pltpu
from jax.sharding import PartitionSpec as P


def face_flux(left, right, speed):
    return 0.5 * speed * (left + right) - 0.5 * jnp.abs(speed) * (right - left)


def remap_advect_kernel(shift_ref, speed_ref, x_ref, o_ref):
    g = pl.program_id(0)
    rows, blocks, cells = x_ref.shape
    lane = lax.broadcasted_iota(jnp.int32, (blocks, cells), 1)
    for i in range(rows):
        r = g * rows + i
        s = shift_ref[r]
        w = speed_ref[r]
        turns = s // cells
        rest = s % cells
        x = x_ref[i]
        y = pltpu.roll(x, rest, 1)
        z = jnp.where(lane >= rest, y, pltpu.roll(y, 1, 0))
        u = pltpu.roll(z, turns, 0)
        l1 = pltpu.roll(u, 1, 1)
        lower = jnp.where(lane == 0, pltpu.roll(l1, 1, 0), l1)
        u1 = pltpu.roll(u, cells - 1, 1)
        upper = jnp.where(lane == cells - 1, pltpu.roll(u1, blocks - 1, 0), u1)
        o_ref[i] = u - (face_flux(u, upper, w) - face_flux(lower, u, w))


def remap_advect(shift, speed, rows_all):
    nr, blocks, cells = rows_all.shape
    rb = 8
    spec = pl.BlockSpec((rb, blocks, cells), lambda g, s, w: (g, 0, 0))
    return pl.pallas_call(
        remap_advect_kernel,
        out_shape=jax.ShapeDtypeStruct(rows_all.shape, rows_all.dtype),
        grid_spec=pltpu.PrefetchScalarGridSpec(
            num_scalar_prefetch=2, grid=(nr // rb,), in_specs=[spec], out_specs=spec
        ),
    )(shift, speed, rows_all)


def per_device(fluid_state, orbit_shift, residual_speed, coupling, radial_solve):
    rows, fields, planes, cells = fluid_state.shape
    nrad = lax.axis_size("rad")
    nazi = lax.axis_size("azi")
    nr = rows * nrad
    nphi = cells * nazi
    zlo = nazi // fields
    zhi = planes // zlo
    x = fluid_state.reshape(rows, fields, zhi, zlo, cells).transpose(2, 1, 3, 0, 4)
    x = x.reshape(zhi * fields * zlo, rows, cells)
    x = lax.all_to_all(x, ("rad", "azi"), split_axis=0, concat_axis=0, tiled=True)
    x = x.reshape(nrad, nazi, rows, cells).transpose(0, 2, 1, 3).reshape(nr, nazi, cells)
    shift = jnp.mod(lax.all_gather(orbit_shift, "rad", tiled=True), nphi).astype(jnp.int32)
    speed = lax.all_gather(residual_speed, "rad", tiled=True)
    adv = remap_advect(shift, speed, x)
    adv = lax.all_to_all(adv, "azi", split_axis=1, concat_axis=1, tiled=True)
    adv = adv.reshape(nr, fields, zlo, cells)
    padded = jnp.pad(adv, ((1, 1), (0, 0), (0, 0), (0, 0)))
    explicit = adv + jnp.einsum(
        "fg,rgzj->rfzj", coupling, padded[2:] - padded[:-2], precision=lax.Precision.HIGHEST
    )
    advanced = jnp.einsum("frk,kfzj->rfzj", radial_solve, explicit, precision=lax.Precision.HIGHEST)
    return lax.all_to_all(advanced, "rad", split_axis=0, concat_axis=2, tiled=True)


def solution(mesh):
    return jax.shard_map(
        per_device,
        mesh=mesh,
        in_specs=(P("rad", None, None, "azi"), P("rad"), P("rad"), P(), P()),
        out_specs=P("rad", None, None, "azi"),
        check_vma=False,
    )
```

```python
import jax
import jax.numpy as jnp
from jax import lax
from jax.experimental import pallas as pl
from jax.experimental.pallas import tpu as pltpu
from jax.sharding import PartitionSpec as P


def face_flux(left, right, speed):
    return 0.5 * speed * (left + right) - 0.5 * jnp.abs(speed) * (right - left)


def remap_advect_kernel(shift_ref, speed_ref, x_ref, o_ref):
    g = pl.program_id(0)
    rows, blocks, cells = x_ref.shape
    lane = lax.broadcasted_iota(jnp.int32, (blocks, cells), 1)

    def body(i, carry):
        r = g * rows + i
        s = shift_ref[r]
        w = speed_ref[r]
        turns = s // cells
        rest = s % cells
        x = x_ref[i]
        y = pltpu.roll(x, rest, 1)
        z = jnp.where(lane >= rest, y, pltpu.roll(y, 1, 0))
        u = pltpu.roll(z, turns, 0)
        l1 = pltpu.roll(u, 1, 1)
        lower = jnp.where(lane == 0, pltpu.roll(l1, 1, 0), l1)
        u1 = pltpu.roll(u, cells - 1, 1)
        upper = jnp.where(lane == cells - 1, pltpu.roll(u1, blocks - 1, 0), u1)
        o_ref[i] = u - (face_flux(u, upper, w) - face_flux(lower, u, w))
        return carry

    lax.fori_loop(0, rows, body, 0)


def remap_advect(shift, speed, rows_all):
    nr, blocks, cells = rows_all.shape
    rb = 8
    spec = pl.BlockSpec((rb, blocks, cells), lambda g, s, w: (g, 0, 0))
    return pl.pallas_call(
        remap_advect_kernel,
        out_shape=jax.ShapeDtypeStruct(rows_all.shape, rows_all.dtype),
        grid_spec=pltpu.PrefetchScalarGridSpec(
            num_scalar_prefetch=2, grid=(nr // rb,), in_specs=[spec], out_specs=spec
        ),
        cost_estimate=pl.CostEstimate(
            flops=30 * rows_all.size, bytes_accessed=8 * rows_all.size, transcendentals=0
        ),
    )(shift, speed, rows_all)


def per_device(fluid_state, orbit_shift, residual_speed, coupling, radial_solve):
    rows, fields, planes, cells = fluid_state.shape
    nrad = lax.axis_size("rad")
    nazi = lax.axis_size("azi")
    nr = rows * nrad
    nphi = cells * nazi
    halves = nazi // fields
    part = rows // halves
    pc = nrad
    chunks = planes // pc
    table = jnp.stack([orbit_shift.astype(jnp.float32), residual_speed])
    table = lax.all_gather(table, "rad", axis=1, tiled=True)
    shift_all = jnp.mod(table[0].astype(jnp.int32), nphi)
    speed_all = table[1]
    h = lax.axis_index("azi") % halves
    order = (jnp.arange(nrad)[:, None] * rows + h * part + jnp.arange(part)[None, :]).reshape(-1)
    shift = shift_all[order]
    speed = speed_all[order]
    outs = []
    for c in range(chunks):
        xc = fluid_state[:, :, c * pc:(c + 1) * pc, :]
        xc = xc.reshape(halves, part, fields, pc, cells).transpose(3, 2, 0, 1, 4)
        xc = xc.reshape(pc * fields * halves, part, cells)
        xc = lax.all_to_all(xc, ("rad", "azi"), split_axis=0, concat_axis=0, tiled=True)
        xc = xc.reshape(nrad, nazi, part, cells).transpose(0, 2, 1, 3).reshape(nrad * part, nazi, cells)
        adv = remap_advect(shift, speed, xc)
        adv = lax.all_to_all(adv, "azi", split_axis=1, concat_axis=1, tiled=True)
        adv = adv.reshape(nrad, part, fields, halves, cells).transpose(0, 3, 1, 2, 4).reshape(nr, fields, cells)
        padded = jnp.pad(adv, ((1, 1), (0, 0), (0, 0)))
        explicit = adv + jnp.einsum(
            "fg,rgj->rfj", coupling, padded[2:] - padded[:-2], precision=lax.Precision.HIGHEST
        )
        advanced = jnp.einsum("frk,kfj->rfj", radial_solve, explicit, precision=lax.Precision.HIGHEST)
        advanced = advanced.reshape(nr, fields, 1, cells)
        outs.append(lax.all_to_all(advanced, "rad", split_axis=0, concat_axis=2, tiled=True))
    return jnp.concatenate(outs, axis=2)


def solution(mesh):
    return jax.shard_map(
        per_device,
        mesh=mesh,
        in_specs=(P("rad", None, None, "azi"), P("rad"), P("rad"), P(), P()),
        out_specs=P("rad", None, None, "azi"),
        check_vma=False,
    )
```

```python
import jax
import jax.numpy as jnp
from jax import lax
from jax.experimental import pallas as pl
from jax.experimental.pallas import tpu as pltpu
from jax.sharding import PartitionSpec as P


def face_flux(left, right, speed):
    return 0.5 * speed * (left + right) - 0.5 * jnp.abs(speed) * (right - left)


def remap_advect_kernel(shift_ref, speed_ref, x_ref, o_ref):
    g = pl.program_id(0)
    rows, blocks, cells = x_ref.shape
    lane = lax.broadcasted_iota(jnp.int32, (blocks, cells), 1)

    def body(i, carry):
        r = g * rows + i
        s = shift_ref[r]
        w = speed_ref[r]
        turns = s // cells
        rest = s % cells
        x = x_ref[i]
        y = pltpu.roll(x, rest, 1)
        z = jnp.where(lane >= rest, y, pltpu.roll(y, 1, 0))
        u = pltpu.roll(z, turns, 0)
        l1 = pltpu.roll(u, 1, 1)
        lower = jnp.where(lane == 0, pltpu.roll(l1, 1, 0), l1)
        u1 = pltpu.roll(u, cells - 1, 1)
        upper = jnp.where(lane == cells - 1, pltpu.roll(u1, blocks - 1, 0), u1)
        o_ref[i] = u - (face_flux(u, upper, w) - face_flux(lower, u, w))
        return carry

    lax.fori_loop(0, rows, body, 0)


def remap_advect(shift, speed, rows_all):
    nr, blocks, cells = rows_all.shape
    rb = 8
    spec = pl.BlockSpec((rb, blocks, cells), lambda g, s, w: (g, 0, 0))
    return pl.pallas_call(
        remap_advect_kernel,
        out_shape=jax.ShapeDtypeStruct(rows_all.shape, rows_all.dtype),
        grid_spec=pltpu.PrefetchScalarGridSpec(
            num_scalar_prefetch=2, grid=(nr // rb,), in_specs=[spec], out_specs=spec
        ),
        cost_estimate=pl.CostEstimate(
            flops=30 * rows_all.size, bytes_accessed=8 * rows_all.size, transcendentals=0
        ),
    )(shift, speed, rows_all)


def per_device(fluid_state, orbit_shift, residual_speed, coupling, radial_solve):
    rows, fields, planes, cells = fluid_state.shape
    nrad = lax.axis_size("rad")
    nazi = lax.axis_size("azi")
    nr = rows * nrad
    nphi = cells * nazi
    halves = nazi // fields
    part = rows // halves
    pc = nrad
    chunks = planes // pc
    table = jnp.stack([orbit_shift.astype(jnp.float32), residual_speed])
    table = lax.all_gather(table, "rad", axis=1, tiled=True)
    shift_all = jnp.mod(table[0].astype(jnp.int32), nphi)
    speed_all = table[1]
    h = lax.axis_index("azi") % halves
    order = (jnp.arange(nrad)[:, None] * rows + h * part + jnp.arange(part)[None, :]).reshape(-1)
    shift = shift_all[order]
    speed = speed_all[order]
    sends = []
    for c in range(chunks):
        xc = fluid_state[:, :, c * pc:(c + 1) * pc, :]
        xc = xc.reshape(halves, part, fields, pc, cells).transpose(3, 2, 0, 1, 4)
        sends.append(xc.reshape(pc * fields * halves, part, cells))
    shift, speed, sends[0] = lax.optimization_barrier((shift, speed, sends[0]))
    outs = []
    for c in range(chunks):
        xc = lax.all_to_all(sends[c], ("rad", "azi"), split_axis=0, concat_axis=0, tiled=True)
        xc = xc.reshape(nrad, nazi, part, cells).transpose(0, 2, 1, 3).reshape(nrad * part, nazi, cells)
        adv = remap_advect(shift, speed, xc)
        adv = lax.all_to_all(adv, "azi", split_axis=1, concat_axis=1, tiled=True)
        adv = adv.reshape(nrad, part, fields, halves, cells).transpose(0, 3, 1, 2, 4).reshape(nr, fields, cells)
        padded = jnp.pad(adv, ((1, 1), (0, 0), (0, 0)))
        explicit = adv + jnp.einsum(
            "fg,rgj->rfj", coupling, padded[2:] - padded[:-2], precision=lax.Precision.HIGHEST
        )
        advanced = jnp.einsum("frk,kfj->rfj", radial_solve, explicit, precision=lax.Precision.HIGHEST)
        advanced = advanced.reshape(nr, fields, 1, cells)
        outs.append(lax.all_to_all(advanced, "rad", split_axis=0, concat_axis=2, tiled=True))
    return jnp.concatenate(outs, axis=2)


def solution(mesh):
    return jax.shard_map(
        per_device,
        mesh=mesh,
        in_specs=(P("rad", None, None, "azi"), P("rad"), P("rad"), P(), P()),
        out_specs=P("rad", None, None, "azi"),
        check_vma=False,
    )
```

```python
import jax
import jax.numpy as jnp
from jax import lax
from jax.experimental import pallas as pl
from jax.experimental.pallas import tpu as pltpu
from jax.sharding import PartitionSpec as P


def face_flux(left, right, speed):
    return 0.5 * speed * (left + right) - 0.5 * jnp.abs(speed) * (right - left)


def remap_advect_kernel(shift_ref, speed_ref, x_ref, o_ref):
    g = pl.program_id(0)
    rows, blocks, cells = x_ref.shape
    lane = lax.broadcasted_iota(jnp.int32, (blocks, cells), 1)

    def body(i, carry):
        r = g * rows + i
        s = shift_ref[r]
        w = speed_ref[r]
        turns = s // cells
        rest = s % cells
        x = x_ref[i]
        y = pltpu.roll(x, rest, 1)
        z = jnp.where(lane >= rest, y, pltpu.roll(y, 1, 0))
        u = pltpu.roll(z, turns, 0)
        l1 = pltpu.roll(u, 1, 1)
        lower = jnp.where(lane == 0, pltpu.roll(l1, 1, 0), l1)
        u1 = pltpu.roll(u, cells - 1, 1)
        upper = jnp.where(lane == cells - 1, pltpu.roll(u1, blocks - 1, 0), u1)
        o_ref[i] = u - (face_flux(u, upper, w) - face_flux(lower, u, w))
        return carry

    lax.fori_loop(0, rows, body, 0)


def remap_advect(shift, speed, rows_all):
    nr, blocks, cells = rows_all.shape
    rb = 8
    spec = pl.BlockSpec((rb, blocks, cells), lambda g, s, w: (g, 0, 0))
    return pl.pallas_call(
        remap_advect_kernel,
        out_shape=jax.ShapeDtypeStruct(rows_all.shape, rows_all.dtype),
        grid_spec=pltpu.PrefetchScalarGridSpec(
            num_scalar_prefetch=2, grid=(nr // rb,), in_specs=[spec], out_specs=spec
        ),
        cost_estimate=pl.CostEstimate(
            flops=30 * rows_all.size, bytes_accessed=8 * rows_all.size, transcendentals=0
        ),
    )(shift, speed, rows_all)


def per_device(fluid_state, orbit_shift, residual_speed, coupling, radial_solve):
    rows, fields, planes, cells = fluid_state.shape
    nrad = lax.axis_size("rad")
    nazi = lax.axis_size("azi")
    nr = rows * nrad
    nphi = cells * nazi
    halves = nazi // fields
    part = rows // halves
    pc = nrad
    chunks = planes // pc
    table = jnp.stack([orbit_shift.astype(jnp.float32), residual_speed])
    got = table[None]
    step = 1
    while step < nrad:
        got = jnp.concatenate(
            [got, lax.ppermute(got, "rad", [(i, (i + step) % nrad) for i in range(nrad)])]
        )
        step *= 2
    me = lax.axis_index("rad")
    table = got[jnp.mod(me - jnp.arange(nrad), nrad)]
    h = lax.axis_index("azi") % halves
    table = lax.dynamic_slice_in_dim(table, h * part, part, axis=2).transpose(1, 0, 2).reshape(2, nrad * part)
    shift = jnp.mod(table[0].astype(jnp.int32), nphi)
    speed = table[1]
    sends = []
    for c in range(chunks):
        xc = fluid_state[:, :, c * pc:(c + 1) * pc, :]
        xc = xc.reshape(halves, part, fields, pc, cells).transpose(3, 2, 0, 1, 4)
        sends.append(xc.reshape(pc * fields * halves, part, cells))
    shift, speed, sends[0] = lax.optimization_barrier((shift, speed, sends[0]))
    outs = []
    for c in range(chunks):
        xc = lax.all_to_all(sends[c], ("rad", "azi"), split_axis=0, concat_axis=0, tiled=True)
        xc = xc.reshape(nrad, nazi, part, cells).transpose(0, 2, 1, 3).reshape(nrad * part, nazi, cells)
        adv = remap_advect(shift, speed, xc)
        adv = lax.all_to_all(adv, "azi", split_axis=1, concat_axis=1, tiled=True)
        adv = adv.reshape(nrad, part, fields, halves, cells).transpose(0, 3, 1, 2, 4).reshape(nr, fields, cells)
        padded = jnp.pad(adv, ((1, 1), (0, 0), (0, 0)))
        explicit = adv + jnp.einsum(
            "fg,rgj->rfj", coupling, padded[2:] - padded[:-2], precision=lax.Precision.HIGHEST
        )
        advanced = jnp.einsum("frk,kfj->rfj", radial_solve, explicit, precision=lax.Precision.HIGHEST)
        advanced = advanced.reshape(nr, fields, 1, cells)
        outs.append(lax.all_to_all(advanced, "rad", split_axis=0, concat_axis=2, tiled=True))
    return jnp.concatenate(outs, axis=2)


def solution(mesh):
    return jax.shard_map(
        per_device,
        mesh=mesh,
        in_specs=(P("rad", None, None, "azi"), P("rad"), P("rad"), P(), P()),
        out_specs=P("rad", None, None, "azi"),
        check_vma=False,
    )
```

```python
import jax
import jax.numpy as jnp
from jax import lax
from jax.experimental import pallas as pl
from jax.experimental.pallas import tpu as pltpu
from jax.sharding import PartitionSpec as P


def face_flux(left, right, speed):
    return 0.5 * speed * (left + right) - 0.5 * jnp.abs(speed) * (right - left)


def remap_advect_kernel(shift_ref, speed_ref, x_ref, o_ref):
    g = pl.program_id(0)
    rows, blocks, cells = x_ref.shape
    lane = lax.broadcasted_iota(jnp.int32, (blocks, cells), 1)

    def body(i, carry):
        r = g * rows + i
        s = shift_ref[r]
        w = speed_ref[r]
        turns = s // cells
        rest = s % cells
        x = x_ref[i]
        y = pltpu.roll(x, rest, 1)
        z = jnp.where(lane >= rest, y, pltpu.roll(y, 1, 0))
        u = pltpu.roll(z, turns, 0)
        l1 = pltpu.roll(u, 1, 1)
        lower = jnp.where(lane == 0, pltpu.roll(l1, 1, 0), l1)
        u1 = pltpu.roll(u, cells - 1, 1)
        upper = jnp.where(lane == cells - 1, pltpu.roll(u1, blocks - 1, 0), u1)
        o_ref[i] = u - (face_flux(u, upper, w) - face_flux(lower, u, w))
        return carry

    lax.fori_loop(0, rows, body, 0)


def remap_advect(shift, speed, rows_all):
    nr, blocks, cells = rows_all.shape
    rb = 8
    spec = pl.BlockSpec((rb, blocks, cells), lambda g, s, w: (g, 0, 0))
    return pl.pallas_call(
        remap_advect_kernel,
        out_shape=jax.ShapeDtypeStruct(rows_all.shape, rows_all.dtype),
        grid_spec=pltpu.PrefetchScalarGridSpec(
            num_scalar_prefetch=2, grid=(nr // rb,), in_specs=[spec], out_specs=spec
        ),
        cost_estimate=pl.CostEstimate(
            flops=30 * rows_all.size, bytes_accessed=8 * rows_all.size, transcendentals=0
        ),
    )(shift, speed, rows_all)


def per_device(fluid_state, orbit_shift, residual_speed, coupling, radial_solve):
    rows, fields, planes, cells = fluid_state.shape
    nrad = lax.axis_size("rad")
    nazi = lax.axis_size("azi")
    nr = rows * nrad
    nphi = cells * nazi
    halves = nazi // fields
    part = rows // halves
    pc = nrad
    chunks = planes // pc
    table = jnp.stack([orbit_shift.astype(jnp.float32), residual_speed])
    got = table[None]
    step = 1
    while step < nrad:
        got = jnp.concatenate(
            [got, lax.ppermute(got, "rad", [(i, (i + step) % nrad) for i in range(nrad)])]
        )
        step *= 2
    me = lax.axis_index("rad")
    table = got[jnp.mod(me - jnp.arange(nrad), nrad)]
    h = lax.axis_index("azi") % halves
    table = lax.dynamic_slice_in_dim(table, h * part, part, axis=2).transpose(1, 0, 2).reshape(2, nrad * part)
    shift = jnp.mod(table[0].astype(jnp.int32), nphi)
    speed = table[1]
    sends = []
    for c in range(chunks):
        xc = fluid_state[:, :, c * pc:(c + 1) * pc, :]
        xc = xc.reshape(halves, part, fields, pc, cells).transpose(3, 2, 0, 1, 4)
        sends.append(xc.reshape(pc * fields * halves, part, cells))
    shift, speed, sends[0] = lax.optimization_barrier((shift, speed, sends[0]))
    outs = []
    for c in range(chunks):
        xc = lax.all_to_all(sends[c], ("rad", "azi"), split_axis=0, concat_axis=0, tiled=True)
        xc = xc.reshape(nrad, nazi, part, cells).transpose(0, 2, 1, 3).reshape(nrad * part, nazi, cells)
        adv = remap_advect(shift, speed, xc)
        adv = lax.all_to_all(adv, "azi", split_axis=1, concat_axis=1, tiled=True)
        adv = adv.reshape(nrad, part, fields, halves, cells).transpose(0, 3, 1, 2, 4).reshape(nr, fields, cells)
        padded = jnp.pad(adv, ((1, 1), (0, 0), (0, 0)))
        explicit = adv + jnp.einsum(
            "fg,rgj->rfj", coupling, padded[2:] - padded[:-2], precision=lax.Precision.HIGHEST
        )
        advanced = jnp.einsum("frk,kfj->rfj", radial_solve, explicit, precision=lax.Precision.HIGHEST)
        got = []
        for k in range(nrad):
            piece = lax.dynamic_slice_in_dim(advanced, jnp.mod(me + k, nrad) * rows, rows, axis=0)
            if k:
                piece = lax.ppermute(piece, "rad", [(i, (i + k) % nrad) for i in range(nrad)])
            got.append(piece)
        outs.append(jnp.stack(got))
    got = jnp.stack(outs)
    got = jnp.take(got, jnp.mod(me - jnp.arange(pc), nrad), axis=1)
    return got.transpose(2, 3, 0, 1, 4).reshape(rows, fields, planes, cells)


def solution(mesh):
    return jax.shard_map(
        per_device,
        mesh=mesh,
        in_specs=(P("rad", None, None, "azi"), P("rad"), P("rad"), P(), P()),
        out_specs=P("rad", None, None, "azi"),
        check_vma=False,
    )
```

```python
import jax
import jax.numpy as jnp
from jax import lax
from jax.experimental import pallas as pl
from jax.experimental.pallas import tpu as pltpu
from jax.sharding import PartitionSpec as P


def face_flux(left, right, speed):
    return 0.5 * speed * (left + right) - 0.5 * jnp.abs(speed) * (right - left)


def remap_advect_kernel(shift_ref, speed_ref, x_ref, o_ref):
    g = pl.program_id(0)
    rows, blocks, cells = x_ref.shape
    lane = lax.broadcasted_iota(jnp.int32, (blocks, cells), 1)

    def body(i, carry):
        r = g * rows + i
        s = shift_ref[r]
        w = speed_ref[r]
        turns = s // cells
        rest = s % cells
        x = x_ref[i]
        y = pltpu.roll(x, rest, 1)
        z = jnp.where(lane >= rest, y, pltpu.roll(y, 1, 0))
        u = pltpu.roll(z, turns, 0)
        l1 = pltpu.roll(u, 1, 1)
        lower = jnp.where(lane == 0, pltpu.roll(l1, 1, 0), l1)
        u1 = pltpu.roll(u, cells - 1, 1)
        upper = jnp.where(lane == cells - 1, pltpu.roll(u1, blocks - 1, 0), u1)
        o_ref[i] = u - (face_flux(u, upper, w) - face_flux(lower, u, w))
        return carry

    lax.fori_loop(0, rows, body, 0)


def remap_advect(shift, speed, rows_all):
    nr, blocks, cells = rows_all.shape
    rb = 8
    spec = pl.BlockSpec((rb, blocks, cells), lambda g, s, w: (g, 0, 0))
    return pl.pallas_call(
        remap_advect_kernel,
        out_shape=jax.ShapeDtypeStruct(rows_all.shape, rows_all.dtype),
        grid_spec=pltpu.PrefetchScalarGridSpec(
            num_scalar_prefetch=2, grid=(nr // rb,), in_specs=[spec], out_specs=spec
        ),
        cost_estimate=pl.CostEstimate(
            flops=30 * rows_all.size, bytes_accessed=8 * rows_all.size, transcendentals=0
        ),
    )(shift, speed, rows_all)


def solve_kernel(w_ref, a_ref, o_ref):
    o_ref[...] = jnp.dot(
        w_ref[...], a_ref[...], precision=lax.Precision.HIGHEST, preferred_element_type=jnp.float32
    )


def solve(weights, adv):
    n, cells = adv.shape
    tile = 256
    return pl.pallas_call(
        solve_kernel,
        out_shape=jax.ShapeDtypeStruct((weights.shape[0], cells), adv.dtype),
        grid=(cells // tile,),
        in_specs=[
            pl.BlockSpec(weights.shape, lambda j: (0, 0)),
            pl.BlockSpec((n, tile), lambda j: (0, j)),
        ],
        out_specs=pl.BlockSpec((weights.shape[0], tile), lambda j: (0, j)),
        cost_estimate=pl.CostEstimate(
            flops=2 * weights.shape[0] * n * cells, bytes_accessed=4 * (weights.size + 2 * adv.size),
            transcendentals=0,
        ),
    )(weights, adv)


def combined_weights(coupling, radial_solve, nrad, rows, halves, part):
    fields, nr, _ = radial_solve.shape
    padded = jnp.pad(radial_solve, ((0, 0), (0, 0), (1, 1)))
    diff = padded[:, :, :-2] - padded[:, :, 2:]
    eye = jnp.eye(fields, dtype=radial_solve.dtype)
    w = eye[:, :, None, None] * radial_solve[:, None] + coupling[:, :, None, None] * diff[:, None]
    w = w.reshape(fields, fields, nr, nrad, halves, part)
    w = w.transpose(2, 0, 1, 4, 3, 5)
    return w.reshape(nr * fields, fields * nr)


def per_device(fluid_state, orbit_shift, residual_speed, coupling, radial_solve):
    rows, fields, planes, cells = fluid_state.shape
    nrad = lax.axis_size("rad")
    nazi = lax.axis_size("azi")
    nr = rows * nrad
    nphi = cells * nazi
    halves = nazi // fields
    part = rows // halves
    pc = nrad
    chunks = planes // pc
    table = jnp.stack([orbit_shift.astype(jnp.float32), residual_speed])
    got = table[None]
    step = 1
    while step < nrad:
        got = jnp.concatenate(
            [got, lax.ppermute(got, "rad", [(i, (i + step) % nrad) for i in range(nrad)])]
        )
        step *= 2
    me = lax.axis_index("rad")
    table = got[jnp.mod(me - jnp.arange(nrad), nrad)]
    h = lax.axis_index("azi") % halves
    table = lax.dynamic_slice_in_dim(table, h * part, part, axis=2).transpose(1, 0, 2).reshape(2, nrad * part)
    shift = jnp.mod(table[0].astype(jnp.int32), nphi)
    speed = table[1]
    sends = []
    for c in range(chunks):
        xc = fluid_state[:, :, c * pc:(c + 1) * pc, :]
        xc = xc.reshape(halves, part, fields, pc, cells).transpose(3, 2, 0, 1, 4)
        sends.append(xc.reshape(pc * fields * halves, part, cells))
    shift, speed, sends[1] = lax.optimization_barrier((shift, speed, sends[1]))
    assert chunks == 2
    weights = combined_weights(coupling, radial_solve, nrad, rows, halves, part)
    outs = []
    for c in range(chunks):
        xc = lax.all_to_all(sends[c], ("rad", "azi"), split_axis=0, concat_axis=0, tiled=True)
        xc = xc.reshape(nrad, nazi, part, cells).transpose(0, 2, 1, 3).reshape(nrad * part, nazi, cells)
        adv = remap_advect(shift, speed, xc).transpose(1, 0, 2)
        adv = lax.all_to_all(adv, "azi", split_axis=0, concat_axis=0, tiled=True)
        advanced = solve(weights, adv.reshape(nazi * nrad * part, cells))
        outs.append(advanced.reshape(nr, fields, cells))
    out = lax.all_to_all(
        outs[1].reshape(nr, fields, 1, cells), "rad", split_axis=0, concat_axis=2, tiled=True
    )
    out = jnp.concatenate([jnp.zeros_like(out), out], axis=2)
    for k in range(nrad):
        piece = lax.dynamic_slice_in_dim(outs[0], jnp.mod(me + k, nrad) * rows, rows, axis=0)
        if k:
            piece = lax.ppermute(piece, "rad", [(i, (i + k) % nrad) for i in range(nrad)])
        out = lax.dynamic_update_slice_in_dim(out, piece[:, :, None, :], jnp.mod(me - k, nrad), axis=2)
    return out


def solution(mesh):
    return jax.shard_map(
        per_device,
        mesh=mesh,
        in_specs=(P("rad", None, None, "azi"), P("rad"), P("rad"), P(), P()),
        out_specs=P("rad", None, None, "azi"),
        check_vma=False,
    )
```

```python
import jax
import jax.numpy as jnp
from jax import lax
from jax.experimental import pallas as pl
from jax.experimental.pallas import tpu as pltpu
from jax.sharding import PartitionSpec as P


def face_flux(left, right, speed):
    return 0.5 * speed * (left + right) - 0.5 * jnp.abs(speed) * (right - left)


def remap_advect_kernel(shift_ref, speed_ref, x_ref, o_ref):
    g = pl.program_id(0)
    rows, blocks, cells = x_ref.shape
    lane = lax.broadcasted_iota(jnp.int32, (blocks, cells), 1)

    def body(i, carry):
        r = g * rows + i
        s = shift_ref[r]
        w = speed_ref[r]
        turns = s // cells
        rest = s % cells
        x = x_ref[i]
        y = pltpu.roll(x, rest, 1)
        z = jnp.where(lane >= rest, y, pltpu.roll(y, 1, 0))
        u = pltpu.roll(z, turns, 0)
        l1 = pltpu.roll(u, 1, 1)
        lower = jnp.where(lane == 0, pltpu.roll(l1, 1, 0), l1)
        u1 = pltpu.roll(u, cells - 1, 1)
        upper = jnp.where(lane == cells - 1, pltpu.roll(u1, blocks - 1, 0), u1)
        o_ref[i] = u - (face_flux(u, upper, w) - face_flux(lower, u, w))
        return carry

    lax.fori_loop(0, rows, body, 0)


def remap_advect(shift, speed, rows_all):
    nr, blocks, cells = rows_all.shape
    rb = 8
    spec = pl.BlockSpec((rb, blocks, cells), lambda g, s, w: (g, 0, 0))
    return pl.pallas_call(
        remap_advect_kernel,
        out_shape=jax.ShapeDtypeStruct(rows_all.shape, rows_all.dtype),
        grid_spec=pltpu.PrefetchScalarGridSpec(
            num_scalar_prefetch=2, grid=(nr // rb,), in_specs=[spec], out_specs=spec
        ),
        cost_estimate=pl.CostEstimate(
            flops=30 * rows_all.size, bytes_accessed=8 * rows_all.size, transcendentals=0
        ),
    )(shift, speed, rows_all)


def solve_kernel(w_ref, a_ref, o_ref):
    o_ref[...] = jnp.dot(
        w_ref[...], a_ref[...], precision=lax.Precision.HIGHEST, preferred_element_type=jnp.float32
    )


def solve(weights, adv):
    n, cells = adv.shape
    tile = 256
    return pl.pallas_call(
        solve_kernel,
        out_shape=jax.ShapeDtypeStruct((weights.shape[0], cells), adv.dtype),
        grid=(cells // tile,),
        in_specs=[
            pl.BlockSpec(weights.shape, lambda j: (0, 0)),
            pl.BlockSpec((n, tile), lambda j: (0, j)),
        ],
        out_specs=pl.BlockSpec((weights.shape[0], tile), lambda j: (0, j)),
        cost_estimate=pl.CostEstimate(
            flops=2 * weights.shape[0] * n * cells, bytes_accessed=4 * (weights.size + 2 * adv.size),
            transcendentals=0,
        ),
    )(weights, adv)


def combined_weights(coupling, radial_solve, nrad, rows, halves, part):
    fields, nr, _ = radial_solve.shape
    padded = jnp.pad(radial_solve, ((0, 0), (0, 0), (1, 1)))
    diff = padded[:, :, :-2] - padded[:, :, 2:]

    def arrange(m):
        m = m.reshape(fields, nr, nrad, halves, part).transpose(1, 0, 3, 2, 4)
        return m.reshape(nr, fields, 1, nr)

    eye = jnp.eye(fields, dtype=radial_solve.dtype)[None, :, :, None]
    w = eye * arrange(radial_solve) + coupling[None, :, :, None] * arrange(diff)
    return w.reshape(nr * fields, fields * nr)


def per_device(fluid_state, orbit_shift, residual_speed, coupling, radial_solve):
    rows, fields, planes, cells = fluid_state.shape
    nrad = lax.axis_size("rad")
    nazi = lax.axis_size("azi")
    nr = rows * nrad
    nphi = cells * nazi
    halves = nazi // fields
    part = rows // halves
    pc = nrad
    chunks = planes // pc
    table = jnp.stack([orbit_shift.astype(jnp.float32), residual_speed])
    got = jnp.stack([table] + [
        lax.ppermute(table, "rad", [(i, (i + k) % nrad) for i in range(nrad)]) for k in range(1, nrad)
    ])
    me = lax.axis_index("rad")
    table = got[jnp.mod(me - jnp.arange(nrad), nrad)]
    h = lax.axis_index("azi") % halves
    table = lax.dynamic_slice_in_dim(table, h * part, part, axis=2).transpose(1, 0, 2).reshape(2, nrad * part)
    shift = jnp.mod(table[0].astype(jnp.int32), nphi)
    speed = table[1]
    sends = []
    for c in range(chunks):
        xc = fluid_state[:, :, c * pc:(c + 1) * pc, :]
        xc = xc.reshape(halves, part, fields, pc, cells).transpose(3, 2, 0, 1, 4)
        sends.append(xc.reshape(pc * fields * halves, part, cells))
    shift, speed, sends[0] = lax.optimization_barrier((shift, speed, sends[0]))
    assert chunks == 2
    weights = combined_weights(coupling, radial_solve, nrad, rows, halves, part)
    outs = []
    for c in range(chunks):
        xc = lax.all_to_all(sends[c], ("rad", "azi"), split_axis=0, concat_axis=0, tiled=True)
        xc = xc.reshape(nrad, nazi, part, cells).transpose(0, 2, 1, 3).reshape(nrad * part, nazi, cells)
        adv = remap_advect(shift, speed, xc).transpose(1, 0, 2)
        adv = lax.all_to_all(adv, "azi", split_axis=0, concat_axis=0, tiled=True)
        advanced = solve(weights, adv.reshape(nazi * nrad * part, cells))
        outs.append(advanced.reshape(nr, fields, cells))
    out = jnp.zeros((rows, fields, planes, cells), outs[0].dtype)
    for c in range(chunks):
        for k in range(nrad):
            piece = lax.dynamic_slice_in_dim(outs[c], jnp.mod(me + k, nrad) * rows, rows, axis=0)
            if k:
                piece = lax.ppermute(piece, "rad", [(i, (i + k) % nrad) for i in range(nrad)])
            out = lax.dynamic_update_slice_in_dim(
                out, piece[:, :, None, :], c * pc + jnp.mod(me - k, nrad), axis=2
            )
    return out


def solution(mesh):
    return jax.shard_map(
        per_device,
        mesh=mesh,
        in_specs=(P("rad", None, None, "azi"), P("rad"), P("rad"), P(), P()),
        out_specs=P("rad", None, None, "azi"),
        check_vma=False,
    )
```

```python
import jax
import jax.numpy as jnp
from jax import lax
from jax.experimental import pallas as pl
from jax.experimental.pallas import tpu as pltpu
from jax.sharding import PartitionSpec as P


def face_flux(left, right, speed):
    return 0.5 * speed * (left + right) - 0.5 * jnp.abs(speed) * (right - left)


def remap_advect_kernel(shift_ref, speed_ref, x_ref, o_ref):
    g = pl.program_id(0)
    rows, blocks, cells = x_ref.shape
    lane = lax.broadcasted_iota(jnp.int32, (blocks, cells), 1)

    def body(i, carry):
        r = g * rows + i
        s = shift_ref[r]
        w = speed_ref[r]
        turns = s // cells
        rest = s % cells
        x = x_ref[i]
        y = pltpu.roll(x, rest, 1)
        z = jnp.where(lane >= rest, y, pltpu.roll(y, 1, 0))
        u = pltpu.roll(z, turns, 0)
        l1 = pltpu.roll(u, 1, 1)
        lower = jnp.where(lane == 0, pltpu.roll(l1, 1, 0), l1)
        u1 = pltpu.roll(u, cells - 1, 1)
        upper = jnp.where(lane == cells - 1, pltpu.roll(u1, blocks - 1, 0), u1)
        o_ref[i] = u - (face_flux(u, upper, w) - face_flux(lower, u, w))
        return carry

    lax.fori_loop(0, rows, body, 0)


def remap_advect(shift, speed, rows_all):
    nr, blocks, cells = rows_all.shape
    rb = 8
    spec = pl.BlockSpec((rb, blocks, cells), lambda g, s, w: (g, 0, 0))
    return pl.pallas_call(
        remap_advect_kernel,
        out_shape=jax.ShapeDtypeStruct(rows_all.shape, rows_all.dtype),
        grid_spec=pltpu.PrefetchScalarGridSpec(
            num_scalar_prefetch=2, grid=(nr // rb,), in_specs=[spec], out_specs=spec
        ),
        cost_estimate=pl.CostEstimate(
            flops=30 * rows_all.size, bytes_accessed=8 * rows_all.size, transcendentals=0
        ),
    )(shift, speed, rows_all)


def solve_kernel(w_ref, a_ref, o_ref):
    o_ref[...] = jnp.dot(
        w_ref[...], a_ref[...], precision=lax.Precision.HIGHEST, preferred_element_type=jnp.float32
    )


def solve(weights, adv):
    n, cells = adv.shape
    tile = 256
    return pl.pallas_call(
        solve_kernel,
        out_shape=jax.ShapeDtypeStruct((weights.shape[0], cells), adv.dtype),
        grid=(cells // tile,),
        in_specs=[
            pl.BlockSpec(weights.shape, lambda j: (0, 0)),
            pl.BlockSpec((n, tile), lambda j: (0, j)),
        ],
        out_specs=pl.BlockSpec((weights.shape[0], tile), lambda j: (0, j)),
        cost_estimate=pl.CostEstimate(
            flops=2 * weights.shape[0] * n * cells, bytes_accessed=4 * (weights.size + 2 * adv.size),
            transcendentals=0,
        ),
    )(weights, adv)


def combined_weights(coupling, radial_solve, nrad, rows, halves, part):
    fields, nr, _ = radial_solve.shape
    padded = jnp.pad(radial_solve, ((0, 0), (0, 0), (1, 1)))
    diff = padded[:, :, :-2] - padded[:, :, 2:]

    def arrange(m):
        m = m.reshape(fields, nr, nrad, halves, part).transpose(1, 0, 3, 2, 4)
        return m.reshape(nr, fields, 1, nr)

    eye = jnp.eye(fields, dtype=radial_solve.dtype)[None, :, :, None]
    w = eye * arrange(radial_solve) + coupling[None, :, :, None] * arrange(diff)
    return w.reshape(nr * fields, fields * nr)


def per_device(fluid_state, orbit_shift, residual_speed, coupling, radial_solve):
    rows, fields, planes, cells = fluid_state.shape
    nrad = lax.axis_size("rad")
    nazi = lax.axis_size("azi")
    nr = rows * nrad
    nphi = cells * nazi
    halves = nazi // fields
    part = rows // halves
    pc = nrad
    chunks = planes // pc
    table = jnp.stack([orbit_shift.astype(jnp.float32), residual_speed])
    got = table[None]
    step = 1
    while step < nrad:
        got = jnp.concatenate(
            [got, lax.ppermute(got, "rad", [(i, (i + step) % nrad) for i in range(nrad)])]
        )
        step *= 2
    me = lax.axis_index("rad")
    table = got[jnp.mod(me - jnp.arange(nrad), nrad)]
    h = lax.axis_index("azi") % halves
    table = lax.dynamic_slice_in_dim(table, h * part, part, axis=2).transpose(1, 0, 2).reshape(2, nrad * part)
    shift = jnp.mod(table[0].astype(jnp.int32), nphi)
    speed = table[1]
    sends = []
    for c in range(chunks):
        xc = fluid_state[:, :, c * pc:(c + 1) * pc, :]
        xc = xc.reshape(halves, part, fields, pc, cells).transpose(3, 2, 0, 1, 4)
        sends.append(xc.reshape(pc * fields * halves, part, cells))
    shift, speed, sends[1] = lax.optimization_barrier((shift, speed, sends[1]))
    assert chunks == 2
    weights = combined_weights(coupling, radial_solve, nrad, rows, halves, part)
    outs = []
    for c in range(chunks):
        xc = lax.all_to_all(sends[c], ("rad", "azi"), split_axis=0, concat_axis=0, tiled=True)
        xc = xc.reshape(nrad, nazi, part, cells).transpose(0, 2, 1, 3).reshape(nrad * part, nazi, cells)
        adv = remap_advect(shift, speed, xc).transpose(1, 0, 2)
        adv = lax.all_to_all(adv, "azi", split_axis=0, concat_axis=0, tiled=True)
        advanced = solve(weights, adv.reshape(nazi * nrad * part, cells))
        outs.append(advanced.reshape(nr, fields, cells))
    out = lax.all_to_all(
        outs[1].reshape(nr, fields, 1, cells), "rad", split_axis=0, concat_axis=2, tiled=True
    )
    out = jnp.concatenate([jnp.zeros_like(out), out], axis=2)
    for k in range(nrad):
        piece = lax.dynamic_slice_in_dim(outs[0], jnp.mod(me + k, nrad) * rows, rows, axis=0)
        if k:
            piece = lax.ppermute(piece, "rad", [(i, (i + k) % nrad) for i in range(nrad)])
        out = lax.dynamic_update_slice_in_dim(out, piece[:, :, None, :], jnp.mod(me - k, nrad), axis=2)
    return out


def solution(mesh):
    return jax.shard_map(
        per_device,
        mesh=mesh,
        in_specs=(P("rad", None, None, "azi"), P("rad"), P("rad"), P(), P()),
        out_specs=P("rad", None, None, "azi"),
        check_vma=False,
    )
```

```python
import jax
import jax.numpy as jnp
from jax import lax
from jax.experimental import pallas as pl
from jax.experimental.pallas import tpu as pltpu
from jax.experimental.layout import Layout, with_layout_constraint
from jax.sharding import PartitionSpec as P


def face_flux(left, right, speed):
    return 0.5 * speed * (left + right) - 0.5 * jnp.abs(speed) * (right - left)


def remap_advect_kernel(shift_ref, speed_ref, x_ref, o_ref):
    g = pl.program_id(0)
    rows, blocks, cells = x_ref.shape
    lane = lax.broadcasted_iota(jnp.int32, (blocks, cells), 1)

    def body(i, carry):
        r = g * rows + i
        s = shift_ref[r]
        w = speed_ref[r]
        turns = s // cells
        rest = s % cells
        x = x_ref[i]
        y = pltpu.roll(x, rest, 1)
        z = jnp.where(lane >= rest, y, pltpu.roll(y, 1, 0))
        u = pltpu.roll(z, turns, 0)
        l1 = pltpu.roll(u, 1, 1)
        lower = jnp.where(lane == 0, pltpu.roll(l1, 1, 0), l1)
        u1 = pltpu.roll(u, cells - 1, 1)
        upper = jnp.where(lane == cells - 1, pltpu.roll(u1, blocks - 1, 0), u1)
        o_ref[i] = u - (face_flux(u, upper, w) - face_flux(lower, u, w))
        return carry

    lax.fori_loop(0, rows, body, 0)


def remap_advect(shift, speed, rows_all):
    nr, blocks, cells = rows_all.shape
    rb = 8
    spec = pl.BlockSpec((rb, blocks, cells), lambda g, s, w: (g, 0, 0))
    return pl.pallas_call(
        remap_advect_kernel,
        out_shape=jax.ShapeDtypeStruct(rows_all.shape, rows_all.dtype),
        grid_spec=pltpu.PrefetchScalarGridSpec(
            num_scalar_prefetch=2, grid=(nr // rb,), in_specs=[spec], out_specs=spec
        ),
        cost_estimate=pl.CostEstimate(
            flops=30 * rows_all.size, bytes_accessed=8 * rows_all.size, transcendentals=0
        ),
    )(shift, speed, rows_all)


def solve_kernel(w_ref, a_ref, o_ref):
    o_ref[...] = jnp.dot(
        w_ref[...], a_ref[...], precision=lax.Precision.HIGHEST, preferred_element_type=jnp.float32
    )


def solve(weights, adv):
    n, cells = adv.shape
    tile = 256
    return pl.pallas_call(
        solve_kernel,
        out_shape=jax.ShapeDtypeStruct((weights.shape[0], cells), adv.dtype),
        grid=(cells // tile,),
        in_specs=[
            pl.BlockSpec(weights.shape, lambda j: (0, 0)),
            pl.BlockSpec((n, tile), lambda j: (0, j)),
        ],
        out_specs=pl.BlockSpec((weights.shape[0], tile), lambda j: (0, j)),
        cost_estimate=pl.CostEstimate(
            flops=2 * weights.shape[0] * n * cells, bytes_accessed=4 * (weights.size + 2 * adv.size),
            transcendentals=0,
        ),
    )(weights, adv)


def combined_weights(coupling, radial_solve, nrad, rows, halves, part):
    fields, nr, _ = radial_solve.shape
    padded = jnp.pad(radial_solve, ((0, 0), (0, 0), (1, 1)))
    diff = padded[:, :, :-2] - padded[:, :, 2:]

    def arrange(m):
        m = m.reshape(fields, nr, nrad, halves, part).transpose(1, 0, 3, 2, 4)
        return m.reshape(nr, fields, 1, nr)

    eye = jnp.eye(fields, dtype=radial_solve.dtype)[None, :, :, None]
    w = eye * arrange(radial_solve) + coupling[None, :, :, None] * arrange(diff)
    return w.reshape(nr * fields, fields * nr)


def per_device(fluid_state, orbit_shift, residual_speed, coupling, radial_solve):
    rows, fields, planes, cells = fluid_state.shape
    nrad = lax.axis_size("rad")
    nazi = lax.axis_size("azi")
    nr = rows * nrad
    nphi = cells * nazi
    halves = nazi // fields
    part = rows // halves
    pc = nrad
    chunks = planes // pc
    table = jnp.stack([orbit_shift.astype(jnp.float32), residual_speed])
    got = table[None]
    step = 1
    while step < nrad:
        got = jnp.concatenate(
            [got, lax.ppermute(got, "rad", [(i, (i + step) % nrad) for i in range(nrad)])]
        )
        step *= 2
    me = lax.axis_index("rad")
    table = got[jnp.mod(me - jnp.arange(nrad), nrad)]
    h = lax.axis_index("azi") % halves
    table = lax.dynamic_slice_in_dim(table, h * part, part, axis=2).transpose(1, 0, 2).reshape(2, nrad * part)
    shift = jnp.mod(table[0].astype(jnp.int32), nphi)
    speed = table[1]
    sends = []
    for c in range(chunks):
        xc = fluid_state[:, :, c * pc:(c + 1) * pc, :]
        xc = xc.reshape(halves, part, fields, pc, cells).transpose(3, 2, 0, 1, 4)
        sends.append(xc.reshape(pc * fields * halves, part, cells))
    shift, speed, sends[1] = lax.optimization_barrier((shift, speed, sends[1]))
    assert chunks == 2
    weights = combined_weights(coupling, radial_solve, nrad, rows, halves, part)
    outs = []
    for c in range(chunks):
        xc = lax.all_to_all(sends[c], ("rad", "azi"), split_axis=0, concat_axis=0, tiled=True)
        xc = xc.reshape(nrad, nazi, part, cells).transpose(0, 2, 1, 3).reshape(nrad * part, nazi, cells)
        adv = remap_advect(shift, speed, xc).transpose(1, 0, 2)
        adv = lax.all_to_all(adv, "azi", split_axis=0, concat_axis=0, tiled=True)
        advanced = solve(weights, adv.reshape(nazi * nrad * part, cells))
        outs.append(advanced.reshape(nr, fields, cells))
    out = jnp.zeros((planes, rows, fields, cells), outs[0].dtype)
    for c in range(chunks):
        for k in range(nrad):
            piece = lax.dynamic_slice_in_dim(outs[c], jnp.mod(me + k, nrad) * rows, rows, axis=0)
            if k:
                piece = lax.ppermute(piece, "rad", [(i, (i + k) % nrad) for i in range(nrad)])
            out = lax.dynamic_update_slice_in_dim(out, piece[None], c * pc + jnp.mod(me - k, nrad), axis=0)
    out = with_layout_constraint(out, Layout(major_to_minor=(0, 1, 2, 3))).transpose(1, 2, 0, 3)
    return out


def solution(mesh):
    return jax.shard_map(
        per_device,
        mesh=mesh,
        in_specs=(P("rad", None, None, "azi"), P("rad"), P("rad"), P(), P()),
        out_specs=P("rad", None, None, "azi"),
        check_vma=False,
    )
```

```python
import jax
import jax.numpy as jnp
from jax import lax
from jax.experimental import pallas as pl
from jax.experimental.pallas import tpu as pltpu
from jax.experimental.layout import Layout, with_layout_constraint
from jax.sharding import PartitionSpec as P


def face_flux(left, right, speed):
    return 0.5 * speed * (left + right) - 0.5 * jnp.abs(speed) * (right - left)


def remap_advect_kernel(shift_ref, speed_ref, x_ref, o_ref):
    g = pl.program_id(0)
    rows, blocks, cells = x_ref.shape
    lane = lax.broadcasted_iota(jnp.int32, (blocks, cells), 1)

    def body(i, carry):
        r = g * rows + i
        s = shift_ref[r]
        w = speed_ref[r]
        turns = s // cells
        rest = s % cells
        x = x_ref[i]
        y = pltpu.roll(x, rest, 1)
        z = jnp.where(lane >= rest, y, pltpu.roll(y, 1, 0))
        u = pltpu.roll(z, turns, 0)
        l1 = pltpu.roll(u, 1, 1)
        lower = jnp.where(lane == 0, pltpu.roll(l1, 1, 0), l1)
        u1 = pltpu.roll(u, cells - 1, 1)
        upper = jnp.where(lane == cells - 1, pltpu.roll(u1, blocks - 1, 0), u1)
        o_ref[i] = u - (face_flux(u, upper, w) - face_flux(lower, u, w))
        return carry

    lax.fori_loop(0, rows, body, 0)


def remap_advect(shift, speed, rows_all):
    nr, blocks, cells = rows_all.shape
    rb = 8
    spec = pl.BlockSpec((rb, blocks, cells), lambda g, s, w: (g, 0, 0))
    return pl.pallas_call(
        remap_advect_kernel,
        out_shape=jax.ShapeDtypeStruct(rows_all.shape, rows_all.dtype),
        grid_spec=pltpu.PrefetchScalarGridSpec(
            num_scalar_prefetch=2, grid=(nr // rb,), in_specs=[spec], out_specs=spec
        ),
        cost_estimate=pl.CostEstimate(
            flops=30 * rows_all.size, bytes_accessed=8 * rows_all.size, transcendentals=0
        ),
    )(shift, speed, rows_all)


def solve_kernel(w_ref, a_ref, o_ref):
    o_ref[...] = jnp.dot(
        w_ref[...], a_ref[...], precision=lax.Precision.HIGHEST, preferred_element_type=jnp.float32
    )


def solve(weights, adv):
    n, cells = adv.shape
    tile = 256
    return pl.pallas_call(
        solve_kernel,
        out_shape=jax.ShapeDtypeStruct((weights.shape[0], cells), adv.dtype),
        grid=(cells // tile,),
        in_specs=[
            pl.BlockSpec(weights.shape, lambda j: (0, 0)),
            pl.BlockSpec((n, tile), lambda j: (0, j)),
        ],
        out_specs=pl.BlockSpec((weights.shape[0], tile), lambda j: (0, j)),
        cost_estimate=pl.CostEstimate(
            flops=2 * weights.shape[0] * n * cells, bytes_accessed=4 * (weights.size + 2 * adv.size),
            transcendentals=0,
        ),
    )(weights, adv)


def combined_weights(coupling, radial_solve, nrad, rows, halves, part):
    fields, nr, _ = radial_solve.shape
    padded = jnp.pad(radial_solve, ((0, 0), (0, 0), (1, 1)))
    diff = padded[:, :, :-2] - padded[:, :, 2:]

    def arrange(m):
        m = m.reshape(fields, nr, nrad, halves, part).transpose(1, 0, 3, 2, 4)
        return m.reshape(nr, fields, 1, nr)

    eye = jnp.eye(fields, dtype=radial_solve.dtype)[None, :, :, None]
    w = eye * arrange(radial_solve) + coupling[None, :, :, None] * arrange(diff)
    return w.reshape(nr * fields, fields * nr)


def per_device(fluid_state, orbit_shift, residual_speed, coupling, radial_solve):
    rows, fields, planes, cells = fluid_state.shape
    nrad = lax.axis_size("rad")
    nazi = lax.axis_size("azi")
    nr = rows * nrad
    nphi = cells * nazi
    halves = nazi // fields
    part = rows // halves
    pc = nrad
    chunks = planes // pc
    me = lax.axis_index("rad")
    h = lax.axis_index("azi") % halves
    sends = []
    for c in range(chunks):
        xc = fluid_state[:, :, c * pc:(c + 1) * pc, :]
        xc = xc.reshape(halves, part, fields, pc, cells).transpose(3, 2, 0, 1, 4)
        sends.append(xc.reshape(pc * fields * halves, part, cells))
    carrier = chunks - 1
    table = jnp.stack([orbit_shift.astype(jnp.float32), residual_speed], axis=1).reshape(halves, part, 2)
    lanes = jnp.zeros((halves, part, 128), jnp.float32).at[:, :, :2].set(table)
    lanes = jnp.broadcast_to(lanes[None, None], (pc, fields, halves, part, 128))
    sends[carrier] = jnp.concatenate([sends[carrier], lanes.reshape(pc * fields * halves, part, 128)], axis=2)
    assert chunks == 2
    weights = combined_weights(coupling, radial_solve, nrad, rows, halves, part)
    got = lax.all_to_all(sends[carrier], ("rad", "azi"), split_axis=0, concat_axis=0, tiled=True)
    table = got[::nazi, :, cells:cells + 2].reshape(nrad * part, 2)
    shift = jnp.mod(table[:, 0].astype(jnp.int32), nphi)
    speed = table[:, 1]
    outs = []
    for c in range(chunks):
        if c == carrier:
            xc = got[:, :, :cells]
        else:
            xc = lax.all_to_all(sends[c], ("rad", "azi"), split_axis=0, concat_axis=0, tiled=True)
        xc = xc.reshape(nrad, nazi, part, cells).transpose(0, 2, 1, 3).reshape(nrad * part, nazi, cells)
        adv = remap_advect(shift, speed, xc).transpose(1, 0, 2)
        adv = lax.all_to_all(adv, "azi", split_axis=0, concat_axis=0, tiled=True)
        advanced = solve(weights, adv.reshape(nazi * nrad * part, cells))
        outs.append(advanced.reshape(nr, fields, cells))
    out = jnp.zeros((planes, rows, fields, cells), outs[0].dtype)
    for c in range(chunks):
        for k in range(nrad):
            piece = lax.dynamic_slice_in_dim(outs[c], jnp.mod(me + k, nrad) * rows, rows, axis=0)
            if k:
                piece = lax.ppermute(piece, "rad", [(i, (i + k) % nrad) for i in range(nrad)])
            out = lax.dynamic_update_slice_in_dim(out, piece[None], c * pc + jnp.mod(me - k, nrad), axis=0)
    out = with_layout_constraint(out, Layout(major_to_minor=(0, 1, 2, 3))).transpose(1, 2, 0, 3)
    return out


def solution(mesh):
    return jax.shard_map(
        per_device,
        mesh=mesh,
        in_specs=(P("rad", None, None, "azi"), P("rad"), P("rad"), P(), P()),
        out_specs=P("rad", None, None, "azi"),
        check_vma=False,
    )
```

```python
import jax
import jax.numpy as jnp
from jax import lax
from jax.experimental import pallas as pl
from jax.experimental.pallas import tpu as pltpu
from jax.sharding import PartitionSpec as P


def face_flux(left, right, speed):
    return 0.5 * speed * (left + right) - 0.5 * jnp.abs(speed) * (right - left)


def remap_advect_kernel(shift_ref, speed_ref, x_ref, o_ref):
    g = pl.program_id(0)
    rows, blocks, cells = x_ref.shape
    lane = lax.broadcasted_iota(jnp.int32, (blocks, cells), 1)

    def body(i, carry):
        r = g * rows + i
        s = shift_ref[r]
        w = speed_ref[r]
        turns = s // cells
        rest = s % cells
        x = x_ref[i]
        y = pltpu.roll(x, rest, 1)
        z = jnp.where(lane >= rest, y, pltpu.roll(y, 1, 0))
        u = pltpu.roll(z, turns, 0)
        l1 = pltpu.roll(u, 1, 1)
        lower = jnp.where(lane == 0, pltpu.roll(l1, 1, 0), l1)
        u1 = pltpu.roll(u, cells - 1, 1)
        upper = jnp.where(lane == cells - 1, pltpu.roll(u1, blocks - 1, 0), u1)
        o_ref[i] = u - (face_flux(u, upper, w) - face_flux(lower, u, w))
        return carry

    lax.fori_loop(0, rows, body, 0)


def remap_advect(shift, speed, rows_all):
    nr, blocks, cells = rows_all.shape
    rb = 8
    spec = pl.BlockSpec((rb, blocks, cells), lambda g, s, w: (g, 0, 0))
    return pl.pallas_call(
        remap_advect_kernel,
        out_shape=jax.ShapeDtypeStruct(rows_all.shape, rows_all.dtype),
        grid_spec=pltpu.PrefetchScalarGridSpec(
            num_scalar_prefetch=2, grid=(nr // rb,), in_specs=[spec], out_specs=spec
        ),
        cost_estimate=pl.CostEstimate(
            flops=30 * rows_all.size, bytes_accessed=8 * rows_all.size, transcendentals=0
        ),
    )(shift, speed, rows_all)


def solve_kernel(w_ref, a_ref, o_ref):
    o_ref[...] = jnp.dot(
        w_ref[...], a_ref[...], precision=lax.Precision.HIGHEST, preferred_element_type=jnp.float32
    )


def solve(weights, adv):
    n, cells = adv.shape
    tile = 256
    return pl.pallas_call(
        solve_kernel,
        out_shape=jax.ShapeDtypeStruct((weights.shape[0], cells), adv.dtype),
        grid=(cells // tile,),
        in_specs=[
            pl.BlockSpec(weights.shape, lambda j: (0, 0)),
            pl.BlockSpec((n, tile), lambda j: (0, j)),
        ],
        out_specs=pl.BlockSpec((weights.shape[0], tile), lambda j: (0, j)),
        cost_estimate=pl.CostEstimate(
            flops=2 * weights.shape[0] * n * cells, bytes_accessed=4 * (weights.size + 2 * adv.size),
            transcendentals=0,
        ),
    )(weights, adv)


def combined_weights(coupling, radial_solve, nrad, rows, halves, part):
    fields, nr, _ = radial_solve.shape
    padded = jnp.pad(radial_solve, ((0, 0), (0, 0), (1, 1)))
    diff = padded[:, :, :-2] - padded[:, :, 2:]

    def arrange(m):
        m = m.reshape(fields, nr, nrad, halves, part).transpose(1, 0, 3, 2, 4)
        return m.reshape(nr, fields, 1, nr)

    eye = jnp.eye(fields, dtype=radial_solve.dtype)[None, :, :, None]
    w = eye * arrange(radial_solve) + coupling[None, :, :, None] * arrange(diff)
    return w.reshape(nr * fields, fields * nr)


def per_device(fluid_state, orbit_shift, residual_speed, coupling, radial_solve):
    rows, fields, planes, cells = fluid_state.shape
    nrad = lax.axis_size("rad")
    nazi = lax.axis_size("azi")
    nr = rows * nrad
    nphi = cells * nazi
    halves = nazi // fields
    part = rows // halves
    pc = nrad
    chunks = planes // pc
    table = jnp.stack([orbit_shift.astype(jnp.float32), residual_speed])
    got = table[None]
    step = 1
    while step < nrad:
        got = jnp.concatenate(
            [got, lax.ppermute(got, "rad", [(i, (i + step) % nrad) for i in range(nrad)])]
        )
        step *= 2
    me = lax.axis_index("rad")
    table = got[jnp.mod(me - jnp.arange(nrad), nrad)]
    h = lax.axis_index("azi") % halves
    table = lax.dynamic_slice_in_dim(table, h * part, part, axis=2).transpose(1, 0, 2).reshape(2, nrad * part)
    shift = jnp.mod(table[0].astype(jnp.int32), nphi)
    speed = table[1]
    sends = []
    for c in range(chunks):
        xc = fluid_state[:, :, c * pc:(c + 1) * pc, :]
        xc = xc.reshape(halves, part, fields, pc, cells).transpose(3, 2, 0, 1, 4)
        sends.append(xc.reshape(pc * fields * halves, part, cells))
    assert chunks == 2
    weights = combined_weights(coupling, radial_solve, nrad, rows, halves, part)
    outs = []
    for c in range(chunks):
        xc = lax.all_to_all(sends[c], ("rad", "azi"), split_axis=0, concat_axis=0, tiled=True)
        xc = xc.reshape(nrad, nazi, part, cells).transpose(0, 2, 1, 3).reshape(nrad * part, nazi, cells)
        adv = remap_advect(shift, speed, xc).transpose(1, 0, 2)
        adv = lax.all_to_all(adv, "azi", split_axis=0, concat_axis=0, tiled=True)
        advanced = solve(weights, adv.reshape(nazi * nrad * part, cells))
        outs.append(advanced.reshape(nr, fields, cells))
    out = lax.all_to_all(
        outs[1].reshape(nr, fields, 1, cells), "rad", split_axis=0, concat_axis=2, tiled=True
    )
    out = jnp.concatenate([jnp.zeros_like(out), out], axis=2)
    for k in range(nrad):
        piece = lax.dynamic_slice_in_dim(outs[0], jnp.mod(me + k, nrad) * rows, rows, axis=0)
        if k:
            piece = lax.ppermute(piece, "rad", [(i, (i + k) % nrad) for i in range(nrad)])
        out = lax.dynamic_update_slice_in_dim(out, piece[:, :, None, :], jnp.mod(me - k, nrad), axis=2)
    return out


def solution(mesh):
    return jax.shard_map(
        per_device,
        mesh=mesh,
        in_specs=(P("rad", None, None, "azi"), P("rad"), P("rad"), P(), P()),
        out_specs=P("rad", None, None, "azi"),
        check_vma=False,
    )
```

```python
import jax
import jax.numpy as jnp
from jax import lax
from jax.experimental import pallas as pl
from jax.experimental.pallas import tpu as pltpu
from jax.experimental.layout import Layout, with_layout_constraint
from jax.sharding import PartitionSpec as P


def face_flux(left, right, speed):
    return 0.5 * speed * (left + right) - 0.5 * jnp.abs(speed) * (right - left)


def remap_advect_kernel(shift_ref, speed_ref, x_ref, o_ref):
    g = pl.program_id(0)
    rows, blocks, cells = x_ref.shape
    lane = lax.broadcasted_iota(jnp.int32, (blocks, cells), 1)

    def body(i, carry):
        r = g * rows + i
        s = shift_ref[r]
        w = speed_ref[r]
        turns = s // cells
        rest = s % cells
        x = x_ref[i]
        y = pltpu.roll(x, rest, 1)
        z = jnp.where(lane >= rest, y, pltpu.roll(y, 1, 0))
        u = pltpu.roll(z, turns, 0)
        l1 = pltpu.roll(u, 1, 1)
        lower = jnp.where(lane == 0, pltpu.roll(l1, 1, 0), l1)
        u1 = pltpu.roll(u, cells - 1, 1)
        upper = jnp.where(lane == cells - 1, pltpu.roll(u1, blocks - 1, 0), u1)
        o_ref[i] = u - (face_flux(u, upper, w) - face_flux(lower, u, w))
        return carry

    lax.fori_loop(0, rows, body, 0)


def remap_advect(shift, speed, rows_all):
    nr, blocks, cells = rows_all.shape
    rb = 8
    spec = pl.BlockSpec((rb, blocks, cells), lambda g, s, w: (g, 0, 0))
    return pl.pallas_call(
        remap_advect_kernel,
        out_shape=jax.ShapeDtypeStruct(rows_all.shape, rows_all.dtype),
        grid_spec=pltpu.PrefetchScalarGridSpec(
            num_scalar_prefetch=2, grid=(nr // rb,), in_specs=[spec], out_specs=spec
        ),
        cost_estimate=pl.CostEstimate(
            flops=30 * rows_all.size, bytes_accessed=8 * rows_all.size, transcendentals=0
        ),
    )(shift, speed, rows_all)


def solve_kernel(w_ref, a_ref, o_ref):
    o_ref[...] = jnp.dot(
        w_ref[...], a_ref[...], precision=lax.Precision.HIGH, preferred_element_type=jnp.float32
    )


def solve(weights, adv):
    n, cells = adv.shape
    tile = 256
    return pl.pallas_call(
        solve_kernel,
        out_shape=jax.ShapeDtypeStruct((weights.shape[0], cells), adv.dtype),
        grid=(cells // tile,),
        in_specs=[
            pl.BlockSpec(weights.shape, lambda j: (0, 0)),
            pl.BlockSpec((n, tile), lambda j: (0, j)),
        ],
        out_specs=pl.BlockSpec((weights.shape[0], tile), lambda j: (0, j)),
        cost_estimate=pl.CostEstimate(
            flops=2 * weights.shape[0] * n * cells, bytes_accessed=4 * (weights.size + 2 * adv.size),
            transcendentals=0,
        ),
    )(weights, adv)


def combined_weights(coupling, radial_solve, nrad, rows, halves, part):
    fields, nr, _ = radial_solve.shape
    padded = jnp.pad(radial_solve, ((0, 0), (0, 0), (1, 1)))
    diff = padded[:, :, :-2] - padded[:, :, 2:]

    def arrange(m):
        m = m.reshape(fields, nr, nrad, halves, part).transpose(1, 0, 3, 2, 4)
        return m.reshape(nr, fields, 1, nr)

    eye = jnp.eye(fields, dtype=radial_solve.dtype)[None, :, :, None]
    w = eye * arrange(radial_solve) + coupling[None, :, :, None] * arrange(diff)
    return w.reshape(nr * fields, fields * nr)


def per_device(fluid_state, orbit_shift, residual_speed, coupling, radial_solve):
    rows, fields, planes, cells = fluid_state.shape
    nrad = lax.axis_size("rad")
    nazi = lax.axis_size("azi")
    nr = rows * nrad
    nphi = cells * nazi
    halves = nazi // fields
    part = rows // halves
    pc = nrad
    chunks = planes // pc
    table = jnp.stack([orbit_shift.astype(jnp.float32), residual_speed])
    got = table[None]
    step = 1
    while step < nrad:
        got = jnp.concatenate(
            [got, lax.ppermute(got, "rad", [(i, (i + step) % nrad) for i in range(nrad)])]
        )
        step *= 2
    me = lax.axis_index("rad")
    table = got[jnp.mod(me - jnp.arange(nrad), nrad)]
    h = lax.axis_index("azi") % halves
    table = lax.dynamic_slice_in_dim(table, h * part, part, axis=2).transpose(1, 0, 2).reshape(2, nrad * part)
    shift = jnp.mod(table[0].astype(jnp.int32), nphi)
    speed = table[1]
    sends = []
    for c in range(chunks):
        xc = fluid_state[:, :, c * pc:(c + 1) * pc, :]
        xc = xc.reshape(halves, part, fields, pc, cells).transpose(3, 2, 0, 1, 4)
        sends.append(xc.reshape(pc * fields * halves, part, cells))
    shift, speed, sends[1] = lax.optimization_barrier((shift, speed, sends[1]))
    assert chunks == 2
    weights = combined_weights(coupling, radial_solve, nrad, rows, halves, part)
    outs = []
    for c in range(chunks):
        xc = lax.all_to_all(sends[c], ("rad", "azi"), split_axis=0, concat_axis=0, tiled=True)
        xc = xc.reshape(nrad, nazi, part, cells).transpose(0, 2, 1, 3).reshape(nrad * part, nazi, cells)
        adv = remap_advect(shift, speed, xc).transpose(1, 0, 2)
        adv = lax.all_to_all(adv, "azi", split_axis=0, concat_axis=0, tiled=True)
        advanced = solve(weights, adv.reshape(nazi * nrad * part, cells))
        outs.append(advanced.reshape(nr, fields, cells))
    out = jnp.zeros((planes, rows, fields, cells), outs[0].dtype)
    for c in range(chunks):
        for k in range(nrad):
            piece = lax.dynamic_slice_in_dim(outs[c], jnp.mod(me + k, nrad) * rows, rows, axis=0)
            if k:
                piece = lax.ppermute(piece, "rad", [(i, (i + k) % nrad) for i in range(nrad)])
            out = lax.dynamic_update_slice_in_dim(out, piece[None], c * pc + jnp.mod(me - k, nrad), axis=0)
    out = with_layout_constraint(out, Layout(major_to_minor=(0, 1, 2, 3))).transpose(1, 2, 0, 3)
    return out


def solution(mesh):
    return jax.shard_map(
        per_device,
        mesh=mesh,
        in_specs=(P("rad", None, None, "azi"), P("rad"), P("rad"), P(), P()),
        out_specs=P("rad", None, None, "azi"),
        check_vma=False,
    )
```

```python
import jax
import jax.numpy as jnp
from jax import lax
from jax.experimental import pallas as pl
from jax.experimental.pallas import tpu as pltpu
from jax.experimental.layout import Layout, with_layout_constraint
from jax.sharding import PartitionSpec as P


def face_flux(left, right, speed):
    return 0.5 * speed * (left + right) - 0.5 * jnp.abs(speed) * (right - left)


def remap_advect_kernel(shift_ref, speed_ref, x_ref, o_ref):
    g = pl.program_id(0)
    rows, blocks, cells = x_ref.shape
    lane = lax.broadcasted_iota(jnp.int32, (blocks, cells), 1)

    def body(i, carry):
        r = g * rows + i
        s = shift_ref[r]
        w = speed_ref[r]
        turns = s // cells
        rest = s % cells
        x = x_ref[i]
        y = pltpu.roll(x, rest, 1)
        z = jnp.where(lane >= rest, y, pltpu.roll(y, 1, 0))
        u = pltpu.roll(z, turns, 0)
        l1 = pltpu.roll(u, 1, 1)
        lower = jnp.where(lane == 0, pltpu.roll(l1, 1, 0), l1)
        u1 = pltpu.roll(u, cells - 1, 1)
        upper = jnp.where(lane == cells - 1, pltpu.roll(u1, blocks - 1, 0), u1)
        o_ref[i] = u - (face_flux(u, upper, w) - face_flux(lower, u, w))
        return carry

    lax.fori_loop(0, rows, body, 0)


def remap_advect(shift, speed, rows_all):
    nr, blocks, cells = rows_all.shape
    rb = 8
    spec = pl.BlockSpec((rb, blocks, cells), lambda g, s, w: (g, 0, 0))
    return pl.pallas_call(
        remap_advect_kernel,
        out_shape=jax.ShapeDtypeStruct(rows_all.shape, rows_all.dtype),
        grid_spec=pltpu.PrefetchScalarGridSpec(
            num_scalar_prefetch=2, grid=(nr // rb,), in_specs=[spec], out_specs=spec
        ),
        cost_estimate=pl.CostEstimate(
            flops=30 * rows_all.size, bytes_accessed=8 * rows_all.size, transcendentals=0
        ),
    )(shift, speed, rows_all)


def solve_kernel(w_ref, a_ref, o_ref):
    o_ref[...] = jnp.dot(
        w_ref[...], a_ref[...], precision=lax.Precision.HIGH, preferred_element_type=jnp.float32
    )


def solve(weights, adv):
    n, cells = adv.shape
    tile = 512
    return pl.pallas_call(
        solve_kernel,
        out_shape=jax.ShapeDtypeStruct((weights.shape[0], cells), adv.dtype),
        grid=(cells // tile,),
        in_specs=[
            pl.BlockSpec(weights.shape, lambda j: (0, 0)),
            pl.BlockSpec((n, tile), lambda j: (0, j)),
        ],
        out_specs=pl.BlockSpec((weights.shape[0], tile), lambda j: (0, j)),
        cost_estimate=pl.CostEstimate(
            flops=2 * weights.shape[0] * n * cells, bytes_accessed=4 * (weights.size + 2 * adv.size),
            transcendentals=0,
        ),
    )(weights, adv)


def combined_weights(coupling, radial_solve, nrad, rows, halves, part):
    fields, nr, _ = radial_solve.shape
    padded = jnp.pad(radial_solve, ((0, 0), (0, 0), (1, 1)))
    diff = padded[:, :, :-2] - padded[:, :, 2:]

    def arrange(m):
        m = m.reshape(fields, nr, nrad, halves, part).transpose(1, 0, 3, 2, 4)
        return m.reshape(nr, fields, 1, nr)

    eye = jnp.eye(fields, dtype=radial_solve.dtype)[None, :, :, None]
    w = eye * arrange(radial_solve) + coupling[None, :, :, None] * arrange(diff)
    return w.reshape(nr * fields, fields * nr)


def per_device(fluid_state, orbit_shift, residual_speed, coupling, radial_solve):
    rows, fields, planes, cells = fluid_state.shape
    nrad = lax.axis_size("rad")
    nazi = lax.axis_size("azi")
    nr = rows * nrad
    nphi = cells * nazi
    halves = nazi // fields
    part = rows // halves
    pc = nrad
    chunks = planes // pc
    table = jnp.stack([orbit_shift.astype(jnp.float32), residual_speed])
    got = table[None]
    step = 1
    while step < nrad:
        got = jnp.concatenate(
            [got, lax.ppermute(got, "rad", [(i, (i + step) % nrad) for i in range(nrad)])]
        )
        step *= 2
    me = lax.axis_index("rad")
    table = got[jnp.mod(me - jnp.arange(nrad), nrad)]
    h = lax.axis_index("azi") % halves
    table = lax.dynamic_slice_in_dim(table, h * part, part, axis=2).transpose(1, 0, 2).reshape(2, nrad * part)
    shift = jnp.mod(table[0].astype(jnp.int32), nphi)
    speed = table[1]
    sends = []
    for c in range(chunks):
        xc = fluid_state[:, :, c * pc:(c + 1) * pc, :]
        xc = xc.reshape(halves, part, fields, pc, cells).transpose(3, 2, 0, 1, 4)
        sends.append(xc.reshape(pc * fields * halves, part, cells))
    shift, speed, sends[1] = lax.optimization_barrier((shift, speed, sends[1]))
    assert chunks == 2
    weights = combined_weights(coupling, radial_solve, nrad, rows, halves, part)
    outs = []
    for c in range(chunks):
        xc = lax.all_to_all(sends[c], ("rad", "azi"), split_axis=0, concat_axis=0, tiled=True)
        xc = xc.reshape(nrad, nazi, part, cells).transpose(0, 2, 1, 3).reshape(nrad * part, nazi, cells)
        adv = remap_advect(shift, speed, xc).transpose(1, 0, 2)
        adv = lax.all_to_all(adv, "azi", split_axis=0, concat_axis=0, tiled=True)
        advanced = solve(weights, adv.reshape(nazi * nrad * part, cells))
        outs.append(advanced.reshape(nr, fields, cells))
    out = jnp.zeros((planes, rows, fields, cells), outs[0].dtype)
    for c in range(chunks):
        for k in range(nrad):
            piece = lax.dynamic_slice_in_dim(outs[c], jnp.mod(me + k, nrad) * rows, rows, axis=0)
            if k:
                piece = lax.ppermute(piece, "rad", [(i, (i + k) % nrad) for i in range(nrad)])
            out = lax.dynamic_update_slice_in_dim(out, piece[None], c * pc + jnp.mod(me - k, nrad), axis=0)
    out = with_layout_constraint(out, Layout(major_to_minor=(0, 1, 2, 3))).transpose(1, 2, 0, 3)
    return out


def solution(mesh):
    return jax.shard_map(
        per_device,
        mesh=mesh,
        in_specs=(P("rad", None, None, "azi"), P("rad"), P("rad"), P(), P()),
        out_specs=P("rad", None, None, "azi"),
        check_vma=False,
    )
```

```python
import jax
import jax.numpy as jnp
from jax import lax
from jax.experimental import pallas as pl
from jax.experimental.pallas import tpu as pltpu
from jax.experimental.layout import Layout, with_layout_constraint
from jax.sharding import PartitionSpec as P


def face_flux(left, right, speed):
    return 0.5 * speed * (left + right) - 0.5 * jnp.abs(speed) * (right - left)


def remap_advect_kernel(shift_ref, speed_ref, x_ref, o_ref):
    g = pl.program_id(0)
    rows, blocks, cells = x_ref.shape
    lane = lax.broadcasted_iota(jnp.int32, (blocks, cells), 1)

    def body(i, carry):
        r = g * rows + i
        s = shift_ref[r]
        w = speed_ref[r]
        turns = s // cells
        rest = s % cells
        x = x_ref[i]
        y = pltpu.roll(x, rest, 1)
        z = jnp.where(lane >= rest, y, pltpu.roll(y, 1, 0))
        u = pltpu.roll(z, turns, 0)
        l1 = pltpu.roll(u, 1, 1)
        lower = jnp.where(lane == 0, pltpu.roll(l1, 1, 0), l1)
        u1 = pltpu.roll(u, cells - 1, 1)
        upper = jnp.where(lane == cells - 1, pltpu.roll(u1, blocks - 1, 0), u1)
        o_ref[i] = u - (face_flux(u, upper, w) - face_flux(lower, u, w))
        return carry

    lax.fori_loop(0, rows, body, 0)


def remap_advect(shift, speed, rows_all):
    nr, blocks, cells = rows_all.shape
    rb = 8
    spec = pl.BlockSpec((rb, blocks, cells), lambda g, s, w: (g, 0, 0))
    return pl.pallas_call(
        remap_advect_kernel,
        out_shape=jax.ShapeDtypeStruct(rows_all.shape, rows_all.dtype),
        grid_spec=pltpu.PrefetchScalarGridSpec(
            num_scalar_prefetch=2, grid=(nr // rb,), in_specs=[spec], out_specs=spec
        ),
        cost_estimate=pl.CostEstimate(
            flops=30 * rows_all.size, bytes_accessed=8 * rows_all.size, transcendentals=0
        ),
    )(shift, speed, rows_all)


def solve_kernel(w_ref, a_ref, o_ref):
    o_ref[...] = jnp.dot(
        w_ref[...], a_ref[...], precision=lax.Precision.HIGH, preferred_element_type=jnp.float32
    )


def solve(weights, adv):
    n, cells = adv.shape
    tile = 256
    return pl.pallas_call(
        solve_kernel,
        out_shape=jax.ShapeDtypeStruct((weights.shape[0], cells), adv.dtype),
        grid=(cells // tile,),
        in_specs=[
            pl.BlockSpec(weights.shape, lambda j: (0, 0)),
            pl.BlockSpec((n, tile), lambda j: (0, j)),
        ],
        out_specs=pl.BlockSpec((weights.shape[0], tile), lambda j: (0, j)),
        cost_estimate=pl.CostEstimate(
            flops=2 * weights.shape[0] * n * cells, bytes_accessed=4 * (weights.size + 2 * adv.size),
            transcendentals=0,
        ),
    )(weights, adv)


def combined_weights(coupling, radial_solve, nrad, rows, halves, part):
    fields, nr, _ = radial_solve.shape
    padded = jnp.pad(radial_solve, ((0, 0), (0, 0), (1, 1)))
    diff = padded[:, :, :-2] - padded[:, :, 2:]

    def arrange(m):
        m = m.reshape(fields, nr, nrad, halves, part).transpose(1, 0, 3, 2, 4)
        return m.reshape(nr, fields, 1, nr)

    eye = jnp.eye(fields, dtype=radial_solve.dtype)[None, :, :, None]
    w = eye * arrange(radial_solve) + coupling[None, :, :, None] * arrange(diff)
    return w.reshape(nr * fields, fields * nr)


def per_device(fluid_state, orbit_shift, residual_speed, coupling, radial_solve):
    rows, fields, planes, cells = fluid_state.shape
    nrad = lax.axis_size("rad")
    nazi = lax.axis_size("azi")
    nr = rows * nrad
    nphi = cells * nazi
    halves = nazi // fields
    part = rows // halves
    pc = nrad
    chunks = planes // pc
    table = jnp.stack([orbit_shift.astype(jnp.float32), residual_speed])
    got = table[None]
    step = 1
    while step < nrad:
        got = jnp.concatenate(
            [got, lax.ppermute(got, "rad", [(i, (i + step) % nrad) for i in range(nrad)])]
        )
        step *= 2
    me = lax.axis_index("rad")
    table = got[jnp.mod(me - jnp.arange(nrad), nrad)]
    h = lax.axis_index("azi") % halves
    table = lax.dynamic_slice_in_dim(table, h * part, part, axis=2).transpose(1, 0, 2).reshape(2, nrad * part)
    shift = jnp.mod(table[0].astype(jnp.int32), nphi)
    speed = table[1]
    sends = []
    for c in range(chunks):
        xc = fluid_state[:, :, c * pc:(c + 1) * pc, :]
        xc = xc.reshape(halves, part, fields, pc, cells).transpose(3, 2, 0, 1, 4)
        sends.append(xc.reshape(pc * fields * halves, part, cells))
    shift, speed, sends[1] = lax.optimization_barrier((shift, speed, sends[1]))
    assert chunks == 2
    weights = combined_weights(coupling, radial_solve, nrad, rows, halves, part)
    outs = []
    for c in range(chunks):
        xc = lax.all_to_all(sends[c], ("rad", "azi"), split_axis=0, concat_axis=0, tiled=True)
        xc = xc.reshape(nrad, nazi, part, cells).transpose(0, 2, 1, 3).reshape(nrad * part, nazi, cells)
        adv = remap_advect(shift, speed, xc).transpose(1, 0, 2)
        adv = lax.all_to_all(adv, "azi", split_axis=0, concat_axis=0, tiled=True)
        advanced = solve(weights, adv.reshape(nazi * nrad * part, cells))
        outs.append(advanced.reshape(nr, fields, cells))
    out = jnp.zeros((planes, rows, fields, cells), outs[0].dtype)
    order = sorted(range(nrad), key=lambda k: -min(k, nrad - k) - (k % 2))[::-1]
    for c in range(chunks):
        for k in order:
            piece = lax.dynamic_slice_in_dim(outs[c], jnp.mod(me + k, nrad) * rows, rows, axis=0)
            if k:
                piece = lax.ppermute(piece, "rad", [(i, (i + k) % nrad) for i in range(nrad)])
            out = lax.dynamic_update_slice_in_dim(out, piece[None], c * pc + jnp.mod(me - k, nrad), axis=0)
    out = with_layout_constraint(out, Layout(major_to_minor=(0, 1, 2, 3))).transpose(1, 2, 0, 3)
    return out


def solution(mesh):
    return jax.shard_map(
        per_device,
        mesh=mesh,
        in_specs=(P("rad", None, None, "azi"), P("rad"), P("rad"), P(), P()),
        out_specs=P("rad", None, None, "azi"),
        check_vma=False,
    )
```

```python
import jax
import jax.numpy as jnp
from jax import lax
from jax.experimental import pallas as pl
from jax.experimental.pallas import tpu as pltpu
from jax.experimental.layout import Layout, with_layout_constraint
from jax.sharding import PartitionSpec as P


def face_flux(left, right, speed):
    return 0.5 * speed * (left + right) - 0.5 * jnp.abs(speed) * (right - left)


def remap_advect_kernel(shift_ref, speed_ref, x_ref, o_ref):
    g = pl.program_id(0)
    rows, blocks, cells = x_ref.shape
    lane = lax.broadcasted_iota(jnp.int32, (blocks, cells), 1)

    def body(i, carry):
        r = g * rows + i
        s = shift_ref[r]
        w = speed_ref[r]
        turns = s // cells
        rest = s % cells
        x = x_ref[i]
        y = pltpu.roll(x, rest, 1)
        z = jnp.where(lane >= rest, y, pltpu.roll(y, 1, 0))
        u = pltpu.roll(z, turns, 0)
        l1 = pltpu.roll(u, 1, 1)
        lower = jnp.where(lane == 0, pltpu.roll(l1, 1, 0), l1)
        u1 = pltpu.roll(u, cells - 1, 1)
        upper = jnp.where(lane == cells - 1, pltpu.roll(u1, blocks - 1, 0), u1)
        o_ref[i] = u - (face_flux(u, upper, w) - face_flux(lower, u, w))
        return carry

    lax.fori_loop(0, rows, body, 0)


def remap_advect(shift, speed, rows_all):
    nr, blocks, cells = rows_all.shape
    rb = 8
    spec = pl.BlockSpec((rb, blocks, cells), lambda g, s, w: (g, 0, 0))
    return pl.pallas_call(
        remap_advect_kernel,
        out_shape=jax.ShapeDtypeStruct(rows_all.shape, rows_all.dtype),
        grid_spec=pltpu.PrefetchScalarGridSpec(
            num_scalar_prefetch=2, grid=(nr // rb,), in_specs=[spec], out_specs=spec
        ),
        cost_estimate=pl.CostEstimate(
            flops=30 * rows_all.size, bytes_accessed=8 * rows_all.size, transcendentals=0
        ),
    )(shift, speed, rows_all)


def solve_kernel(w_ref, a_ref, o_ref):
    o_ref[...] = jnp.dot(
        w_ref[...], a_ref[...], precision=lax.Precision.HIGH, preferred_element_type=jnp.float32
    )


def solve(weights, adv):
    n, cells = adv.shape
    tile = 256
    return pl.pallas_call(
        solve_kernel,
        out_shape=jax.ShapeDtypeStruct((weights.shape[0], cells), adv.dtype),
        grid=(cells // tile,),
        in_specs=[
            pl.BlockSpec(weights.shape, lambda j: (0, 0)),
            pl.BlockSpec((n, tile), lambda j: (0, j)),
        ],
        out_specs=pl.BlockSpec((weights.shape[0], tile), lambda j: (0, j)),
        cost_estimate=pl.CostEstimate(
            flops=2 * weights.shape[0] * n * cells, bytes_accessed=4 * (weights.size + 2 * adv.size),
            transcendentals=0,
        ),
    )(weights, adv)


def combined_weights(coupling, radial_solve, nrad, rows, halves, part):
    fields, nr, _ = radial_solve.shape
    padded = jnp.pad(radial_solve, ((0, 0), (0, 0), (1, 1)))
    diff = padded[:, :, :-2] - padded[:, :, 2:]

    def arrange(m):
        m = m.reshape(fields, nr, nrad, halves, part).transpose(1, 0, 3, 2, 4)
        return m.reshape(nr, fields, 1, nr)

    eye = jnp.eye(fields, dtype=radial_solve.dtype)[None, :, :, None]
    w = eye * arrange(radial_solve) + coupling[None, :, :, None] * arrange(diff)
    return w.reshape(nr * fields, fields * nr)


def per_device(fluid_state, orbit_shift, residual_speed, coupling, radial_solve):
    rows, fields, planes, cells = fluid_state.shape
    nrad = lax.axis_size("rad")
    nazi = lax.axis_size("azi")
    nr = rows * nrad
    nphi = cells * nazi
    halves = nazi // fields
    part = rows // halves
    pc = nrad
    chunks = planes // pc
    table = jnp.stack([orbit_shift.astype(jnp.float32), residual_speed])
    got = table[None]
    step = 1
    while step < nrad:
        got = jnp.concatenate(
            [got, lax.ppermute(got, "rad", [(i, (i + step) % nrad) for i in range(nrad)])]
        )
        step *= 2
    me = lax.axis_index("rad")
    table = got[jnp.mod(me - jnp.arange(nrad), nrad)]
    h = lax.axis_index("azi") % halves
    table = lax.dynamic_slice_in_dim(table, h * part, part, axis=2).transpose(1, 0, 2).reshape(2, nrad * part)
    shift = jnp.mod(table[0].astype(jnp.int32), nphi)
    speed = table[1]
    sends = []
    for c in range(chunks):
        xc = fluid_state[:, :, c * pc:(c + 1) * pc, :]
        xc = xc.reshape(halves, part, fields, pc, cells).transpose(3, 2, 0, 1, 4)
        sends.append(xc.reshape(pc * fields * halves, part, cells))
    shift, speed, sends[1] = lax.optimization_barrier((shift, speed, sends[1]))
    assert chunks == 2
    weights = combined_weights(coupling, radial_solve, nrad, rows, halves, part)
    outs = []
    for c in range(chunks):
        xc = lax.all_to_all(sends[c], ("rad", "azi"), split_axis=0, concat_axis=0, tiled=True)
        xc = xc.reshape(nrad, nazi, part, cells).transpose(0, 2, 1, 3).reshape(nrad * part, nazi, cells)
        adv = remap_advect(shift, speed, xc).transpose(1, 0, 2)
        adv = lax.all_to_all(adv, "azi", split_axis=0, concat_axis=0, tiled=True)
        advanced = solve(weights, adv.reshape(nazi * nrad * part, cells))
        outs.append(advanced.reshape(nr, fields, cells))
    out = jnp.zeros((planes, rows, fields, cells), outs[0].dtype)
    order = [0, 6, 2, 7, 1, 4, 5, 3][:nrad] if nrad == 8 else list(range(nrad))
    for c in range(chunks):
        for k in order:
            piece = lax.dynamic_slice_in_dim(outs[c], jnp.mod(me + k, nrad) * rows, rows, axis=0)
            if k:
                piece = lax.ppermute(piece, "rad", [(i, (i + k) % nrad) for i in range(nrad)])
            out = lax.dynamic_update_slice_in_dim(out, piece[None], c * pc + jnp.mod(me - k, nrad), axis=0)
    out = with_layout_constraint(out, Layout(major_to_minor=(0, 1, 2, 3))).transpose(1, 2, 0, 3)
    return out


def solution(mesh):
    return jax.shard_map(
        per_device,
        mesh=mesh,
        in_specs=(P("rad", None, None, "azi"), P("rad"), P("rad"), P(), P()),
        out_specs=P("rad", None, None, "azi"),
        check_vma=False,
    )
```

```python
import jax
import jax.numpy as jnp
from jax import lax
from jax.experimental import pallas as pl
from jax.experimental.pallas import tpu as pltpu
from jax.experimental.layout import Layout, with_layout_constraint
from jax.sharding import PartitionSpec as P


def face_flux(left, right, speed):
    return 0.5 * speed * (left + right) - 0.5 * jnp.abs(speed) * (right - left)


def remap_advect_kernel(shift_ref, speed_ref, x_ref, o_ref):
    g = pl.program_id(0)
    rows, blocks, cells = x_ref.shape
    lane = lax.broadcasted_iota(jnp.int32, (blocks, cells), 1)

    def body(i, carry):
        r = g * rows + i
        s = shift_ref[r]
        w = speed_ref[r]
        turns = s // cells
        rest = s % cells
        x = x_ref[i]
        y = pltpu.roll(x, rest, 1)
        z = jnp.where(lane >= rest, y, pltpu.roll(y, 1, 0))
        u = pltpu.roll(z, turns, 0)
        l1 = pltpu.roll(u, 1, 1)
        lower = jnp.where(lane == 0, pltpu.roll(l1, 1, 0), l1)
        u1 = pltpu.roll(u, cells - 1, 1)
        upper = jnp.where(lane == cells - 1, pltpu.roll(u1, blocks - 1, 0), u1)
        o_ref[i] = u - (face_flux(u, upper, w) - face_flux(lower, u, w))
        return carry

    lax.fori_loop(0, rows, body, 0)


def remap_advect(shift, speed, rows_all):
    nr, blocks, cells = rows_all.shape
    rb = 8
    spec = pl.BlockSpec((rb, blocks, cells), lambda g, s, w: (g, 0, 0))
    return pl.pallas_call(
        remap_advect_kernel,
        out_shape=jax.ShapeDtypeStruct(rows_all.shape, rows_all.dtype),
        grid_spec=pltpu.PrefetchScalarGridSpec(
            num_scalar_prefetch=2, grid=(nr // rb,), in_specs=[spec], out_specs=spec
        ),
        cost_estimate=pl.CostEstimate(
            flops=30 * rows_all.size, bytes_accessed=8 * rows_all.size, transcendentals=0
        ),
    )(shift, speed, rows_all)


def solve_kernel(w_ref, a_ref, o_ref):
    o_ref[...] = jnp.dot(
        w_ref[...], a_ref[...], precision=lax.Precision.HIGH, preferred_element_type=jnp.float32
    )


def solve(weights, adv):
    n, cells = adv.shape
    tile = 256
    return pl.pallas_call(
        solve_kernel,
        out_shape=jax.ShapeDtypeStruct((weights.shape[0], cells), adv.dtype),
        grid=(cells // tile,),
        in_specs=[
            pl.BlockSpec(weights.shape, lambda j: (0, 0)),
            pl.BlockSpec((n, tile), lambda j: (0, j)),
        ],
        out_specs=pl.BlockSpec((weights.shape[0], tile), lambda j: (0, j)),
        cost_estimate=pl.CostEstimate(
            flops=2 * weights.shape[0] * n * cells, bytes_accessed=4 * (weights.size + 2 * adv.size),
            transcendentals=0,
        ),
    )(weights, adv)


def combined_weights(coupling, radial_solve, nrad, rows, halves, part):
    fields, nr, _ = radial_solve.shape
    padded = jnp.pad(radial_solve, ((0, 0), (0, 0), (1, 1)))
    diff = padded[:, :, :-2] - padded[:, :, 2:]

    def arrange(m):
        m = m.reshape(fields, nr, nrad, halves, part).transpose(1, 0, 3, 2, 4)
        return m.reshape(nr, fields, 1, nr)

    eye = jnp.eye(fields, dtype=radial_solve.dtype)[None, :, :, None]
    w = eye * arrange(radial_solve) + coupling[None, :, :, None] * arrange(diff)
    return w.reshape(nr * fields, fields * nr)


def per_device(fluid_state, orbit_shift, residual_speed, coupling, radial_solve):
    rows, fields, planes, cells = fluid_state.shape
    nrad = lax.axis_size("rad")
    nazi = lax.axis_size("azi")
    nr = rows * nrad
    nphi = cells * nazi
    halves = nazi // fields
    part = rows // halves
    pc = nrad
    chunks = planes // pc
    table = jnp.stack([orbit_shift.astype(jnp.float32), residual_speed])
    got = table[None]
    step = 1
    while step < nrad:
        got = jnp.concatenate(
            [got, lax.ppermute(got, "rad", [(i, (i + step) % nrad) for i in range(nrad)])]
        )
        step *= 2
    me = lax.axis_index("rad")
    table = got[jnp.mod(me - jnp.arange(nrad), nrad)]
    h = lax.axis_index("azi") % halves
    table = lax.dynamic_slice_in_dim(table, h * part, part, axis=2).transpose(1, 0, 2).reshape(2, nrad * part)
    shift = jnp.mod(table[0].astype(jnp.int32), nphi)
    speed = table[1]
    sends = []
    for c in range(chunks):
        xc = fluid_state[:, :, c * pc:(c + 1) * pc, :]
        xc = xc.reshape(halves, part, fields, pc, cells).transpose(3, 2, 0, 1, 4)
        sends.append(xc.reshape(pc * fields * halves, part, cells))
    shift, speed, sends[1] = lax.optimization_barrier((shift, speed, sends[1]))
    assert chunks == 2
    weights = combined_weights(coupling, radial_solve, nrad, rows, halves, part)
    weights = jnp.roll(weights, -me * rows * fields, axis=0)
    outs = []
    for c in range(chunks):
        xc = lax.all_to_all(sends[c], ("rad", "azi"), split_axis=0, concat_axis=0, tiled=True)
        xc = xc.reshape(nrad, nazi, part, cells).transpose(0, 2, 1, 3).reshape(nrad * part, nazi, cells)
        adv = remap_advect(shift, speed, xc).transpose(1, 0, 2)
        adv = lax.all_to_all(adv, "azi", split_axis=0, concat_axis=0, tiled=True)
        advanced = solve(weights, adv.reshape(nazi * nrad * part, cells))
        outs.append(advanced.reshape(nr, fields, cells))
    out = jnp.zeros((planes, rows, fields, cells), outs[0].dtype)
    order = sorted(range(nrad), key=lambda k: -min(k, nrad - k) - (k % 2))[::-1]
    for c in range(chunks):
        for k in order:
            piece = outs[c][k * rows:(k + 1) * rows]
            if k:
                piece = lax.ppermute(piece, "rad", [(i, (i + k) % nrad) for i in range(nrad)])
            out = lax.dynamic_update_slice_in_dim(out, piece[None], c * pc + jnp.mod(me - k, nrad), axis=0)
    out = with_layout_constraint(out, Layout(major_to_minor=(0, 1, 2, 3))).transpose(1, 2, 0, 3)
    return out


def solution(mesh):
    return jax.shard_map(
        per_device,
        mesh=mesh,
        in_specs=(P("rad", None, None, "azi"), P("rad"), P("rad"), P(), P()),
        out_specs=P("rad", None, None, "azi"),
        check_vma=False,
    )
```

```python
import jax
import jax.numpy as jnp
from jax import lax
from jax.experimental import pallas as pl
from jax.experimental.pallas import tpu as pltpu
from jax.experimental.layout import Layout, with_layout_constraint
from jax.sharding import PartitionSpec as P


def face_flux(left, right, speed):
    return 0.5 * speed * (left + right) - 0.5 * jnp.abs(speed) * (right - left)


def remap_advect_kernel(shift_ref, speed_ref, x_ref, o_ref):
    g = pl.program_id(0)
    rows, blocks, cells = x_ref.shape
    lane = lax.broadcasted_iota(jnp.int32, (blocks, cells), 1)

    def body(i, carry):
        r = g * rows + i
        s = shift_ref[r]
        w = speed_ref[r]
        turns = s // cells
        rest = s % cells
        x = x_ref[i]
        y = pltpu.roll(x, rest, 1)
        z = jnp.where(lane >= rest, y, pltpu.roll(y, 1, 0))
        u = pltpu.roll(z, turns, 0)
        l1 = pltpu.roll(u, 1, 1)
        lower = jnp.where(lane == 0, pltpu.roll(l1, 1, 0), l1)
        u1 = pltpu.roll(u, cells - 1, 1)
        upper = jnp.where(lane == cells - 1, pltpu.roll(u1, blocks - 1, 0), u1)
        o_ref[i] = u - (face_flux(u, upper, w) - face_flux(lower, u, w))
        return carry

    lax.fori_loop(0, rows, body, 0)


def remap_advect(shift, speed, rows_all):
    nr, blocks, cells = rows_all.shape
    rb = 8
    spec = pl.BlockSpec((rb, blocks, cells), lambda g, s, w: (g, 0, 0))
    return pl.pallas_call(
        remap_advect_kernel,
        out_shape=jax.ShapeDtypeStruct(rows_all.shape, rows_all.dtype),
        grid_spec=pltpu.PrefetchScalarGridSpec(
            num_scalar_prefetch=2, grid=(nr // rb,), in_specs=[spec], out_specs=spec
        ),
        cost_estimate=pl.CostEstimate(
            flops=30 * rows_all.size, bytes_accessed=8 * rows_all.size, transcendentals=0
        ),
    )(shift, speed, rows_all)


def solve_kernel(w_ref, a_ref, o_ref):
    o_ref[...] = jnp.dot(
        w_ref[...], a_ref[...], precision=lax.Precision.HIGH, preferred_element_type=jnp.float32
    )


def solve(weights, adv):
    n, cells = adv.shape
    tile = 512
    return pl.pallas_call(
        solve_kernel,
        out_shape=jax.ShapeDtypeStruct((weights.shape[0], cells), adv.dtype),
        grid=(cells // tile,),
        in_specs=[
            pl.BlockSpec(weights.shape, lambda j: (0, 0)),
            pl.BlockSpec((n, tile), lambda j: (0, j)),
        ],
        out_specs=pl.BlockSpec((weights.shape[0], tile), lambda j: (0, j)),
        cost_estimate=pl.CostEstimate(
            flops=2 * weights.shape[0] * n * cells, bytes_accessed=4 * (weights.size + 2 * adv.size),
            transcendentals=0,
        ),
    )(weights, adv)


def combined_weights(coupling, radial_solve, nrad, rows, halves, part):
    fields, nr, _ = radial_solve.shape
    padded = jnp.pad(radial_solve, ((0, 0), (0, 0), (1, 1)))
    diff = padded[:, :, :-2] - padded[:, :, 2:]

    def arrange(m):
        m = m.reshape(fields, nr, nrad, halves, part).transpose(1, 0, 3, 2, 4)
        return m.reshape(nr, fields, 1, nr)

    eye = jnp.eye(fields, dtype=radial_solve.dtype)[None, :, :, None]
    w = eye * arrange(radial_solve) + coupling[None, :, :, None] * arrange(diff)
    return w.reshape(nr * fields, fields * nr)


def per_device(fluid_state, orbit_shift, residual_speed, coupling, radial_solve):
    rows, fields, planes, cells = fluid_state.shape
    nrad = lax.axis_size("rad")
    nazi = lax.axis_size("azi")
    nr = rows * nrad
    nphi = cells * nazi
    halves = nazi // fields
    part = rows // halves
    pc = nrad
    chunks = planes // pc
    table = jnp.stack([orbit_shift.astype(jnp.float32), residual_speed])
    got = table[None]
    step = 1
    while step < nrad:
        got = jnp.concatenate(
            [got, lax.ppermute(got, "rad", [(i, (i + step) % nrad) for i in range(nrad)])]
        )
        step *= 2
    me = lax.axis_index("rad")
    table = got[jnp.mod(me - jnp.arange(nrad), nrad)]
    h = lax.axis_index("azi") % halves
    table = lax.dynamic_slice_in_dim(table, h * part, part, axis=2).transpose(1, 0, 2).reshape(2, nrad * part)
    shift = jnp.mod(table[0].astype(jnp.int32), nphi)
    speed = table[1]
    sends = []
    for c in range(chunks):
        xc = fluid_state[:, :, c * pc:(c + 1) * pc, :]
        xc = xc.reshape(halves, part, fields, pc, cells).transpose(3, 2, 0, 1, 4)
        sends.append(xc.reshape(pc * fields * halves, part, cells))
    shift, speed, sends[1] = lax.optimization_barrier((shift, speed, sends[1]))
    assert chunks == 2
    weights = combined_weights(coupling, radial_solve, nrad, rows, halves, part)
    weights = jnp.roll(weights, -me * rows * fields, axis=0)
    outs = []
    for c in range(chunks):
        xc = lax.all_to_all(sends[c], ("rad", "azi"), split_axis=0, concat_axis=0, tiled=True)
        xc = xc.reshape(nrad, nazi, part, cells).transpose(0, 2, 1, 3).reshape(nrad * part, nazi, cells)
        adv = remap_advect(shift, speed, xc).transpose(1, 0, 2)
        adv = lax.all_to_all(adv, "azi", split_axis=0, concat_axis=0, tiled=True)
        advanced = solve(weights, adv.reshape(nazi * nrad * part, cells))
        outs.append(advanced.reshape(nr, fields, cells))
    out = jnp.zeros((planes, rows, fields, cells), outs[0].dtype)
    order = sorted(range(nrad), key=lambda k: -min(k, nrad - k) - (k % 2))[::-1]
    for c in range(chunks):
        for k in order:
            piece = outs[c][k * rows:(k + 1) * rows]
            if k:
                piece = lax.ppermute(piece, "rad", [(i, (i + k) % nrad) for i in range(nrad)])
            out = lax.dynamic_update_slice_in_dim(out, piece[None], c * pc + jnp.mod(me - k, nrad), axis=0)
    out = with_layout_constraint(out, Layout(major_to_minor=(0, 1, 2, 3))).transpose(1, 2, 0, 3)
    return out


def solution(mesh):
    return jax.shard_map(
        per_device,
        mesh=mesh,
        in_specs=(P("rad", None, None, "azi"), P("rad"), P("rad"), P(), P()),
        out_specs=P("rad", None, None, "azi"),
        check_vma=False,
    )
```

```python
import jax
import jax.numpy as jnp
from jax import lax
from jax.experimental import pallas as pl
from jax.experimental.pallas import tpu as pltpu
from jax.experimental.layout import Layout, with_layout_constraint
from jax.sharding import PartitionSpec as P


def face_flux(left, right, speed):
    return 0.5 * speed * (left + right) - 0.5 * jnp.abs(speed) * (right - left)


def remap_advect_kernel(shift_ref, speed_ref, x_ref, o_ref):
    g = pl.program_id(0)
    rows, blocks, cells = x_ref.shape
    lane = lax.broadcasted_iota(jnp.int32, (blocks, cells), 1)

    def body(i, carry):
        r = g * rows + i
        s = shift_ref[r]
        w = speed_ref[r]
        turns = s // cells
        rest = s % cells
        x = x_ref[i]
        y = pltpu.roll(x, rest, 1)
        z = jnp.where(lane >= rest, y, pltpu.roll(y, 1, 0))
        u = pltpu.roll(z, turns, 0)
        l1 = pltpu.roll(u, 1, 1)
        lower = jnp.where(lane == 0, pltpu.roll(l1, 1, 0), l1)
        u1 = pltpu.roll(u, cells - 1, 1)
        upper = jnp.where(lane == cells - 1, pltpu.roll(u1, blocks - 1, 0), u1)
        o_ref[i] = u - (face_flux(u, upper, w) - face_flux(lower, u, w))
        return carry

    lax.fori_loop(0, rows, body, 0)


def remap_advect(shift, speed, rows_all):
    nr, blocks, cells = rows_all.shape
    rb = 8
    spec = pl.BlockSpec((rb, blocks, cells), lambda g, s, w: (g, 0, 0))
    return pl.pallas_call(
        remap_advect_kernel,
        out_shape=jax.ShapeDtypeStruct(rows_all.shape, rows_all.dtype),
        grid_spec=pltpu.PrefetchScalarGridSpec(
            num_scalar_prefetch=2, grid=(nr // rb,), in_specs=[spec], out_specs=spec
        ),
        cost_estimate=pl.CostEstimate(
            flops=30 * rows_all.size, bytes_accessed=8 * rows_all.size, transcendentals=0
        ),
    )(shift, speed, rows_all)


def solve_kernel(w_ref, a_ref, o_ref):
    o_ref[...] = jnp.dot(
        w_ref[...], a_ref[...], precision=lax.Precision.HIGH, preferred_element_type=jnp.float32
    )


def solve(weights, adv):
    n, cells = adv.shape
    tile = 1024
    return pl.pallas_call(
        solve_kernel,
        out_shape=jax.ShapeDtypeStruct((weights.shape[0], cells), adv.dtype),
        grid=(cells // tile,),
        in_specs=[
            pl.BlockSpec(weights.shape, lambda j: (0, 0)),
            pl.BlockSpec((n, tile), lambda j: (0, j)),
        ],
        out_specs=pl.BlockSpec((weights.shape[0], tile), lambda j: (0, j)),
        cost_estimate=pl.CostEstimate(
            flops=2 * weights.shape[0] * n * cells, bytes_accessed=4 * (weights.size + 2 * adv.size),
            transcendentals=0,
        ),
    )(weights, adv)


def combined_weights(coupling, radial_solve, nrad, rows, halves, part):
    fields, nr, _ = radial_solve.shape
    padded = jnp.pad(radial_solve, ((0, 0), (0, 0), (1, 1)))
    diff = padded[:, :, :-2] - padded[:, :, 2:]

    def arrange(m):
        m = m.reshape(fields, nr, nrad, halves, part).transpose(1, 0, 3, 2, 4)
        return m.reshape(nr, fields, 1, nr)

    eye = jnp.eye(fields, dtype=radial_solve.dtype)[None, :, :, None]
    w = eye * arrange(radial_solve) + coupling[None, :, :, None] * arrange(diff)
    return w.reshape(nr * fields, fields * nr)


def per_device(fluid_state, orbit_shift, residual_speed, coupling, radial_solve):
    rows, fields, planes, cells = fluid_state.shape
    nrad = lax.axis_size("rad")
    nazi = lax.axis_size("azi")
    nr = rows * nrad
    nphi = cells * nazi
    halves = nazi // fields
    part = rows // halves
    pc = nrad
    chunks = planes // pc
    table = jnp.stack([orbit_shift.astype(jnp.float32), residual_speed])
    got = table[None]
    step = 1
    while step < nrad:
        got = jnp.concatenate(
            [got, lax.ppermute(got, "rad", [(i, (i + step) % nrad) for i in range(nrad)])]
        )
        step *= 2
    me = lax.axis_index("rad")
    table = got[jnp.mod(me - jnp.arange(nrad), nrad)]
    h = lax.axis_index("azi") % halves
    table = lax.dynamic_slice_in_dim(table, h * part, part, axis=2).transpose(1, 0, 2).reshape(2, nrad * part)
    shift = jnp.mod(table[0].astype(jnp.int32), nphi)
    speed = table[1]
    sends = []
    for c in range(chunks):
        xc = fluid_state[:, :, c * pc:(c + 1) * pc, :]
        xc = xc.reshape(halves, part, fields, pc, cells).transpose(3, 2, 0, 1, 4)
        sends.append(xc.reshape(pc * fields * halves, part, cells))
    shift, speed, sends[1] = lax.optimization_barrier((shift, speed, sends[1]))
    assert chunks == 2
    weights = combined_weights(coupling, radial_solve, nrad, rows, halves, part)
    weights = jnp.roll(weights, -me * rows * fields, axis=0)
    outs = []
    for c in range(chunks):
        xc = lax.all_to_all(sends[c], ("rad", "azi"), split_axis=0, concat_axis=0, tiled=True)
        xc = xc.reshape(nrad, nazi, part, cells).transpose(0, 2, 1, 3).reshape(nrad * part, nazi, cells)
        adv = remap_advect(shift, speed, xc).transpose(1, 0, 2)
        adv = lax.all_to_all(adv, "azi", split_axis=0, concat_axis=0, tiled=True)
        advanced = solve(weights, adv.reshape(nazi * nrad * part, cells))
        outs.append(advanced.reshape(nr, fields, cells))
    out = jnp.zeros((planes, rows, fields, cells), outs[0].dtype)
    order = sorted(range(nrad), key=lambda k: -min(k, nrad - k) - (k % 2))[::-1]
    for c in range(chunks):
        for k in order:
            piece = outs[c][k * rows:(k + 1) * rows]
            if k:
                piece = lax.ppermute(piece, "rad", [(i, (i + k) % nrad) for i in range(nrad)])
            out = lax.dynamic_update_slice_in_dim(out, piece[None], c * pc + jnp.mod(me - k, nrad), axis=0)
    out = with_layout_constraint(out, Layout(major_to_minor=(0, 1, 2, 3))).transpose(1, 2, 0, 3)
    return out


def solution(mesh):
    return jax.shard_map(
        per_device,
        mesh=mesh,
        in_specs=(P("rad", None, None, "azi"), P("rad"), P("rad"), P(), P()),
        out_specs=P("rad", None, None, "azi"),
        check_vma=False,
    )
```
